256 devices in a mesh: grp: 16 (over x_hi, y, core), dom: 16 (over z, x_lo).
Axes of the slice: x: 4 (x_hi: 2, x_lo: 2; x = x_hi * 2 + x_lo), y: 4, z: 8, core: 2. Of those that a mesh axis runs over, the one named last changes fastest.
Arguments:
- positions: float32 [11264, 4096], P('grp', 'dom'), may hold values from 0 to 32
- energies: float32 [11264, 4096], P('grp', 'dom'), may hold values from -6 to 6
- bucket: int32 [11264], P('grp'), may hold values from 0 to 8191, as said below
- impedance: float32 [3, 2, 128, 128, 256], P(None, None, 'dom', 'grp'), may hold values from -6 to 6
- history: float32 [2, 2, 128, 128, 256], P(None, None, 'dom', 'grp'), may hold values from -1.8 to 1.8
Outputs:
- positions_out: float32 [11264, 4096], P('grp', 'dom')
- energies_out: float32 [11264, 4096], P('grp', 'dom')
- spectrum: float32 [2, 128, 128, 256], P(None, 'dom', 'grp')
The draws below stay inside these ranges and needn't reach their ends.
Inputs may be any that keep to these rules, and one draw needn't show every extreme that they name: Within one train group no two bunches share a bucket; the first bunch of each group sits in bucket 0 and its last bunch in bucket 8192 - 1.
All inputs are finite; a program needn't handle non-finite values.
Results may differ from the reference program's by a relative error of at most 0.00013.
Values sent between devices are 32-bit elements; how exact they have to be, the bound alone decides.
No kernel may reach another device: no remote copies, remote signals or barrier semaphores. Data moves between devices by JAX's collectives and lax.ppermute only.
A program may use at most 64 MiB of HBM per device.

```python
import math
import jax
import jax.numpy as jnp
from jax import lax

BINS = 32
N3 = 256
HIST = 2
BUNCH_GRP = 704
N1 = 128
N2 = 128
M = 4194304
BUCK_GRP = 8192
BUNCHES = 11264
PART = 4096
N_GRP = 16


def draw_bucket(key, part):

    def one_group(subkey):
        inner = jax.random.permutation(subkey, BUCK_GRP - 2)[:BUNCH_GRP - 2].astype(jnp.int32) + 1
        first = jnp.zeros((1,), jnp.int32)
        final = jnp.full((1,), BUCK_GRP - 1, jnp.int32)
        return jnp.concatenate([first, inner, final])
    subkeys = jax.random.split(jax.random.fold_in(key, 7), BUNCHES // BUNCH_GRP)
    return jax.vmap(one_group)(subkeys).reshape(-1)


def shard_levels(stream_key, extent, shards, smallest, high):
    def one(dim, shards_of):
        heights = jax.random.uniform(jax.random.fold_in(jax.random.fold_in(stream_key, 6), dim), (shards_of,), jnp.float32, smallest / len(shards), high / len(shards))
        return jnp.repeat(jnp.exp(heights), extent[dim] // shards_of).reshape((-1,) + (1,) * (len(extent) - dim - 1))

    gain = one(*shards[0])
    for cut in shards[1:]:
        gain = gain * one(*cut)
    return gain


def bell_draw(rng, shape, deviation, most, shards=(), kind=jnp.bfloat16):
    values = jax.random.normal(rng, shape, jnp.float32) * deviation
    if len(shards) > 0:
        values = shard_levels(rng, shape, shards, -0.22, 0.18) * values
    return jnp.clip(values, min=-most, max=most).astype(kind)


def setup_inputs(seed: int = 0) -> dict:
    key_of = jax.random.split(jax.random.key(seed), 6)
    return {
        "positions": jnp.clip(32.0 * jax.random.uniform(key_of[0], (BUNCHES, PART), jnp.float32) ** shard_levels(key_of[0], (BUNCHES, PART), ((0, 16), (1, 16)), -0.2, 0.2), 0.0, 32.0),
        "energies": bell_draw(key_of[1], (BUNCHES, PART), 1.0, 6.0, ((0, 16), (1, 16)), jnp.float32),
        "bucket": draw_bucket(jax.random.fold_in(key_of[5], 71), 0),
        "impedance": bell_draw(key_of[3], (HIST + 1, 2, N1, N2, N3), 1.0, 6.0, ((2, 16), (3, 16)), jnp.float32),
        "history": bell_draw(key_of[4], (HIST, 2, N1, N2, N3), 0.3, 1.8, ((2, 16), (3, 16)), jnp.float32),
    }


def kernel_table(places):
    centers = jnp.arange(BINS, dtype=places.dtype) + 0.5
    offset = places[:, None, :] - centers[None, :, None]
    return jnp.exp(-0.5 * offset * offset)

def to_grid(values):
    return values.reshape(N3, N2, N1).transpose(2, 1, 0)

def reference(positions, energies, bucket, impedance, history):
    place_blocks = positions.reshape(BUNCHES // 16, 16, PART)

    def block_profile(place_block):
        return lax.optimization_barrier(jnp.sum(kernel_table(place_block), axis=2)) / PART
    profile = lax.map(block_profile, place_blocks).reshape(BUNCHES, BINS)
    group_of = jnp.arange(BUNCHES, dtype=jnp.int32) // BUNCH_GRP
    cycle_bucket = (group_of * BUCK_GRP + bucket).astype(jnp.int32)
    density = jnp.zeros((BUCK_GRP * N_GRP, BINS), profile.dtype).at[cycle_bucket].add(profile).reshape(-1)
    transform = jnp.fft.fft(density) / math.sqrt(BUNCHES)
    spec_real = to_grid(jnp.real(transform))
    spec_imag = to_grid(jnp.imag(transform))
    spectrum = jnp.stack([spec_real, spec_imag])
    volt_real = impedance[0, 0] * spec_real - impedance[0, 1] * spec_imag
    volt_imag = impedance[0, 0] * spec_imag + impedance[0, 1] * spec_real
    for earlier in range(HIST):
        past_real = history[earlier, 0]
        past_imag = history[earlier, 1]
        volt_real = volt_real + impedance[earlier + 1, 0] * past_real - impedance[earlier + 1, 1] * past_imag
        volt_imag = volt_imag + impedance[earlier + 1, 0] * past_imag + impedance[earlier + 1, 1] * past_real
    induced = volt_real.transpose(2, 1, 0).reshape(-1) + 1j * volt_imag.transpose(2, 1, 0).reshape(-1)
    voltage = jnp.real(jnp.fft.ifft(induced)) * math.sqrt(M)
    volt_rows = voltage.reshape(-1, BINS)[cycle_bucket]

    def kick_block(inputs):
        place_block, volt_block = inputs
        table_block = kernel_table(place_block)
        weighted = jnp.einsum('bjp,bj->bp', table_block, volt_block, precision=lax.Precision.HIGHEST)
        return weighted / lax.optimization_barrier(jnp.sum(table_block, axis=1))
    kick_volts = lax.map(kick_block, (place_blocks, volt_rows.reshape(BUNCHES // 16, 16, BINS))).reshape(BUNCHES, PART)
    energies_out = energies - 0.5 * jnp.sin(2.0 * math.pi * (positions - 0.5 * BINS) / BINS) - kick_volts
    positions_out = positions + 0.25 * energies_out
    return (positions_out, energies_out, spectrum)
```

```python
import math

import jax
import jax.numpy as jnp
from jax import lax
from jax.sharding import PartitionSpec as P

BINS = 32
N3 = 256
R1 = 8
R2 = 8
HIST = 2
BUNCH_GRP = 704
P_DEV = 256


highest = lax.Precision.HIGHEST
two_pi = 2.0 * math.pi


def kernel_table(places):
    centers = jnp.arange(BINS, dtype=jnp.float32) + 0.5
    offset = places[:, None, :] - centers[None, :, None]
    return jnp.exp(-0.5 * offset * offset)


def dft_tables(length):
    series = jnp.arange(length, dtype=jnp.int32)
    windings = series[:, None] * series[None, :] % length
    angles = windings.astype(jnp.float32) * (two_pi / length)
    return (jnp.cos(angles), jnp.sin(angles))


def rotation(windings, modulus):
    angles = (windings % modulus).astype(jnp.float32) * (two_pi / modulus)
    return (jnp.cos(angles), jnp.sin(angles))


def contract(pattern, operand, matrix):
    return jnp.einsum(pattern, operand, matrix, precision=highest)


def dom_sum(rows, domains):
    chunk = rows.shape[0] // domains
    pieces = lax.all_to_all(rows.reshape(domains, chunk, BINS), "dom", 0, 0, tiled=True)
    mine = jnp.sum(pieces, axis=0)
    spread = jnp.broadcast_to(mine[None], (domains, chunk, BINS))
    return lax.all_to_all(spread, "dom", 0, 0, tiled=True).reshape(rows.shape)


def on_device(positions, energies, bucket, impedance, history):
    groups = lax.axis_size("grp")
    domains = lax.axis_size("dom")
    group_index = lax.axis_index("grp")
    domain_index = lax.axis_index("dom")
    first_len = R1 * groups
    second_len = R2 * domains
    cycle_len = first_len * second_len * N3
    plane_len = second_len * N3
    depth_len = N3 // groups
    first_part = first_len // domains
    second_part = second_len // groups
    per_row = N3 // BINS
    row_buckets = second_len * per_row
    own_rows = R2 * per_row
    partial_value = jnp.sum(kernel_table(positions), axis=2) / float(P_DEV * domains)
    first_row = bucket // row_buckets
    within = bucket % row_buckets
    owner_dom = within // own_rows
    owned_here = owner_dom == domain_index
    slot = jnp.where(owned_here, first_row * own_rows + within - owner_dom * own_rows, -1)
    picker = (slot[None, :] == jnp.arange(R1 * own_rows, dtype=jnp.int32)[:, None]).astype(jnp.float32)
    totals = dom_sum(partial_value, domains)
    line_slab = contract("sb,bj->sj", picker, totals)
    density = line_slab.reshape(R1, R2, N3)
    cos_first, sin_first = dft_tables(first_len)
    cos_second, sin_second = dft_tables(second_len)
    cos_third, sin_third = dft_tables(N3)
    received = lax.all_to_all(density, "grp", split_axis=2, concat_axis=0, tiled=True)
    real_out = contract("nab,kn->abk", received, cos_first)
    imag_out = -contract("nab,kn->abk", received, sin_first)
    rows_real = real_out
    rows_imag = imag_out
    second_global = domain_index * R2 + jnp.arange(R2, dtype=jnp.int32)
    depth_global = group_index * depth_len + jnp.arange(depth_len, dtype=jnp.int32)
    first_freq = jnp.arange(first_len, dtype=jnp.int32)
    cos_turn, sin_turn = rotation(
        first_freq[None, None, :]
        * (second_global[:, None, None] * N3 + depth_global[None, :, None]),
        cycle_len,
    )
    twist_real = rows_real * cos_turn + rows_imag * sin_turn
    twist_imag = rows_imag * cos_turn - rows_real * sin_turn
    part_real, part_imag = lax.all_to_all(
        jnp.stack([twist_real, twist_imag]), "dom", split_axis=3, concat_axis=1, tiled=True
    )
    real_out = contract("nbk,mn->bkm", part_real, cos_second) + contract(
        "nbk,mn->bkm", part_imag, sin_second
    )
    imag_out = contract("nbk,mn->bkm", part_imag, cos_second) - contract(
        "nbk,mn->bkm", part_real, sin_second
    )
    cols_real = real_out
    cols_imag = imag_out
    second_freq = jnp.arange(second_len, dtype=jnp.int32)
    cos_turn, sin_turn = rotation(
        depth_global[:, None, None] * second_freq[None, None, :], plane_len
    )
    turned_real = cols_real * cos_turn + cols_imag * sin_turn
    turned_imag = cols_imag * cos_turn - cols_real * sin_turn
    part_real, part_imag = lax.all_to_all(
        jnp.stack([turned_real, turned_imag]), "grp", split_axis=3, concat_axis=1, tiled=True
    )
    real_out = contract("nac,kn->ack", part_real, cos_third) + contract(
        "nac,kn->ack", part_imag, sin_third
    )
    imag_out = contract("nac,kn->ack", part_imag, cos_third) - contract(
        "nac,kn->ack", part_real, sin_third
    )
    full_real = real_out
    full_imag = imag_out
    norm_factor = 1.0 / math.sqrt(BUNCH_GRP * groups)
    spec_real = full_real * norm_factor
    spec_imag = full_imag * norm_factor
    spectrum = jnp.stack([spec_real, spec_imag])
    volt_real = impedance[0, 0] * spec_real - impedance[0, 1] * spec_imag
    volt_imag = impedance[0, 0] * spec_imag + impedance[0, 1] * spec_real
    for earlier in range(HIST):
        past_real = history[earlier, 0]
        past_imag = history[earlier, 1]
        volt_real = (
            volt_real
            + impedance[earlier + 1, 0] * past_real
            - impedance[earlier + 1, 1] * past_imag
        )
        volt_imag = (
            volt_imag
            + impedance[earlier + 1, 0] * past_imag
            + impedance[earlier + 1, 1] * past_real
        )
    back_real = contract("ack,nk->acn", volt_real, cos_third) - contract(
        "ack,nk->acn", volt_imag, sin_third
    )
    back_imag = contract("ack,nk->acn", volt_real, sin_third) + contract(
        "ack,nk->acn", volt_imag, cos_third
    )
    second_own = group_index * second_part + jnp.arange(second_part, dtype=jnp.int32)
    depth_all = jnp.arange(N3, dtype=jnp.int32)
    cos_turn, sin_turn = rotation(second_own[None, :, None] * depth_all[None, None, :], plane_len)
    lift_real = back_real * cos_turn - back_imag * sin_turn
    lift_imag = back_real * sin_turn + back_imag * cos_turn
    part_real, part_imag = lax.all_to_all(
        jnp.stack([lift_real, lift_imag]), "grp", split_axis=3, concat_axis=2, tiled=True
    )
    real_out = contract("akb,nk->anb", part_real, cos_second) - contract(
        "akb,nk->anb", part_imag, sin_second
    )
    imag_out = contract("akb,nk->anb", part_real, sin_second) + contract(
        "akb,nk->anb", part_imag, cos_second
    )
    first_own = domain_index * first_part + jnp.arange(first_part, dtype=jnp.int32)
    cos_turn, sin_turn = rotation(
        first_own[:, None, None] * (second_freq[None, :, None] * N3 + depth_global[None, None, :]),
        cycle_len,
    )
    spin_real = real_out * cos_turn - imag_out * sin_turn
    spin_imag = real_out * sin_turn + imag_out * cos_turn
    inverse_factor = 1.0 / math.sqrt(cycle_len)
    part_real, part_imag = lax.all_to_all(
        jnp.stack([spin_real, spin_imag]), "dom", split_axis=2, concat_axis=1, tiled=True
    )
    summed = contract("kab,nk->nab", part_real, cos_first) - contract(
        "kab,nk->nab", part_imag, sin_first
    )
    volt_part = summed * inverse_factor
    volt_slab = lax.all_to_all(volt_part, "grp", split_axis=0, concat_axis=2, tiled=True).reshape(
        R1 * own_rows, BINS
    )
    owned_volts = contract("sb,sj->bj", picker, volt_slab)
    volt_rows = dom_sum(owned_volts, domains)
    table = kernel_table(positions)
    weighted = jnp.sum(table * volt_rows[:, :, None], axis=1)
    kick_volts = weighted / jnp.sum(table, axis=1)
    energies_out = energies - 0.5 * jnp.sin(two_pi * (positions - 0.5 * BINS) / BINS) - kick_volts
    positions_out = positions + 0.25 * energies_out
    return (positions_out, energies_out, spectrum)


def solution(mesh):
    placed = (
        P("grp", "dom"),
        P("grp", "dom"),
        P("grp"),
        P(None, None, "dom", "grp", None),
        P(None, None, "dom", "grp", None),
    )
    return jax.shard_map(
        on_device,
        mesh=mesh,
        in_specs=placed,
        out_specs=(P("grp", "dom"), P("grp", "dom"), P(None, "dom", "grp", None)),
        check_vma=False,
    )
```

```python
import math

import jax
import jax.numpy as jnp
from jax import lax
from jax.sharding import PartitionSpec as P
from jax.experimental import pallas as pl
from jax.experimental.pallas import tpu as pltpu

BINS = 32
N3 = 256
R1 = 8
R2 = 8
HIST = 2
BUNCH_GRP = 704
P_DEV = 256


highest = lax.Precision.HIGHEST
two_pi = 2.0 * math.pi


def kernel_table(places):
    centers = jnp.arange(BINS, dtype=jnp.float32) + 0.5
    offset = places[:, None, :] - centers[None, :, None]
    return jnp.exp(-0.5 * offset * offset)


def dft_tables(length):
    series = jnp.arange(length, dtype=jnp.int32)
    windings = series[:, None] * series[None, :] % length
    angles = windings.astype(jnp.float32) * (two_pi / length)
    return (jnp.cos(angles), jnp.sin(angles))


def rotation(windings, modulus):
    angles = (windings % modulus).astype(jnp.float32) * (two_pi / modulus)
    return (jnp.cos(angles), jnp.sin(angles))


def contract(pattern, operand, matrix):
    return jnp.einsum(pattern, operand, matrix, precision=highest)


def dom_sum(rows, domains):
    chunk = rows.shape[0] // domains
    pieces = lax.all_to_all(rows.reshape(domains, chunk, BINS), "dom", 0, 0, tiled=True)
    mine = jnp.sum(pieces, axis=0)
    spread = jnp.broadcast_to(mine[None], (domains, chunk, BINS))
    return lax.all_to_all(spread, "dom", 0, 0, tiled=True).reshape(rows.shape)


KICK_ROWS = 64
SUB_ROWS = 8


def kick_kernel(pos_ref, drift_ref, volt_ref, pos_out, en_out):
    def sub_block(i, carry):
        rows = pl.ds(pl.multiple_of(i * SUB_ROWS, SUB_ROWS), SUB_ROWS)
        place = pos_ref[rows, :]
        volts = volt_ref[rows, :]
        weighted = jnp.zeros_like(place)
        norm = jnp.zeros_like(place)
        for j in range(BINS):
            offset = place - (j + 0.5)
            table = jnp.exp(-0.5 * offset * offset)
            weighted = weighted + table * volts[:, j : j + 1]
            norm = norm + table
        energy = drift_ref[rows, :] - weighted / norm
        en_out[rows, :] = energy
        pos_out[rows, :] = place + 0.25 * energy
        return carry

    lax.fori_loop(0, KICK_ROWS // SUB_ROWS, sub_block, 0)


def kick_call(positions, drifted, volt_rows):
    bunches, width = positions.shape
    wide = pl.BlockSpec((KICK_ROWS, width), lambda i: (i, 0))
    narrow = pl.BlockSpec((KICK_ROWS, BINS), lambda i: (i, 0))
    shape = jax.ShapeDtypeStruct(positions.shape, jnp.float32)
    return pl.pallas_call(
        kick_kernel,
        grid=(bunches // KICK_ROWS,),
        in_specs=[wide, wide, narrow],
        out_specs=[wide, wide],
        out_shape=[shape, shape],
        cost_estimate=pl.CostEstimate(
            flops=12 * bunches * width * BINS,
            transcendentals=bunches * width * BINS,
            bytes_accessed=4 * bunches * (4 * width + BINS),
        ),
    )(positions, drifted, volt_rows)


def on_device(positions, energies, bucket, impedance, history):
    groups = lax.axis_size("grp")
    domains = lax.axis_size("dom")
    group_index = lax.axis_index("grp")
    domain_index = lax.axis_index("dom")
    first_len = R1 * groups
    second_len = R2 * domains
    cycle_len = first_len * second_len * N3
    plane_len = second_len * N3
    depth_len = N3 // groups
    first_part = first_len // domains
    second_part = second_len // groups
    per_row = N3 // BINS
    row_buckets = second_len * per_row
    own_rows = R2 * per_row
    partial_value = jnp.sum(kernel_table(positions), axis=2) / float(P_DEV * domains)
    first_row = bucket // row_buckets
    within = bucket % row_buckets
    owner_dom = within // own_rows
    owned_here = owner_dom == domain_index
    slot = jnp.where(owned_here, first_row * own_rows + within - owner_dom * own_rows, -1)
    picker = (slot[None, :] == jnp.arange(R1 * own_rows, dtype=jnp.int32)[:, None]).astype(jnp.float32)
    totals = dom_sum(partial_value, domains)
    line_slab = contract("sb,bj->sj", picker, totals)
    density = line_slab.reshape(R1, R2, N3)
    cos_first, sin_first = dft_tables(first_len)
    cos_second, sin_second = dft_tables(second_len)
    cos_third, sin_third = dft_tables(N3)
    received = lax.all_to_all(density, "grp", split_axis=2, concat_axis=0, tiled=True)
    real_out = contract("nab,kn->abk", received, cos_first)
    imag_out = -contract("nab,kn->abk", received, sin_first)
    rows_real = real_out
    rows_imag = imag_out
    second_global = domain_index * R2 + jnp.arange(R2, dtype=jnp.int32)
    depth_global = group_index * depth_len + jnp.arange(depth_len, dtype=jnp.int32)
    first_freq = jnp.arange(first_len, dtype=jnp.int32)
    cos_turn, sin_turn = rotation(
        first_freq[None, None, :]
        * (second_global[:, None, None] * N3 + depth_global[None, :, None]),
        cycle_len,
    )
    twist_real = rows_real * cos_turn + rows_imag * sin_turn
    twist_imag = rows_imag * cos_turn - rows_real * sin_turn
    part_real, part_imag = lax.all_to_all(
        jnp.stack([twist_real, twist_imag]), "dom", split_axis=3, concat_axis=1, tiled=True
    )
    real_out = contract("nbk,mn->bkm", part_real, cos_second) + contract(
        "nbk,mn->bkm", part_imag, sin_second
    )
    imag_out = contract("nbk,mn->bkm", part_imag, cos_second) - contract(
        "nbk,mn->bkm", part_real, sin_second
    )
    cols_real = real_out
    cols_imag = imag_out
    second_freq = jnp.arange(second_len, dtype=jnp.int32)
    cos_turn, sin_turn = rotation(
        depth_global[:, None, None] * second_freq[None, None, :], plane_len
    )
    turned_real = cols_real * cos_turn + cols_imag * sin_turn
    turned_imag = cols_imag * cos_turn - cols_real * sin_turn
    part_real, part_imag = lax.all_to_all(
        jnp.stack([turned_real, turned_imag]), "grp", split_axis=3, concat_axis=1, tiled=True
    )
    real_out = contract("nac,kn->ack", part_real, cos_third) + contract(
        "nac,kn->ack", part_imag, sin_third
    )
    imag_out = contract("nac,kn->ack", part_imag, cos_third) - contract(
        "nac,kn->ack", part_real, sin_third
    )
    full_real = real_out
    full_imag = imag_out
    norm_factor = 1.0 / math.sqrt(BUNCH_GRP * groups)
    spec_real = full_real * norm_factor
    spec_imag = full_imag * norm_factor
    spectrum = jnp.stack([spec_real, spec_imag])
    volt_real = impedance[0, 0] * spec_real - impedance[0, 1] * spec_imag
    volt_imag = impedance[0, 0] * spec_imag + impedance[0, 1] * spec_real
    for earlier in range(HIST):
        past_real = history[earlier, 0]
        past_imag = history[earlier, 1]
        volt_real = (
            volt_real
            + impedance[earlier + 1, 0] * past_real
            - impedance[earlier + 1, 1] * past_imag
        )
        volt_imag = (
            volt_imag
            + impedance[earlier + 1, 0] * past_imag
            + impedance[earlier + 1, 1] * past_real
        )
    back_real = contract("ack,nk->acn", volt_real, cos_third) - contract(
        "ack,nk->acn", volt_imag, sin_third
    )
    back_imag = contract("ack,nk->acn", volt_real, sin_third) + contract(
        "ack,nk->acn", volt_imag, cos_third
    )
    second_own = group_index * second_part + jnp.arange(second_part, dtype=jnp.int32)
    depth_all = jnp.arange(N3, dtype=jnp.int32)
    cos_turn, sin_turn = rotation(second_own[None, :, None] * depth_all[None, None, :], plane_len)
    lift_real = back_real * cos_turn - back_imag * sin_turn
    lift_imag = back_real * sin_turn + back_imag * cos_turn
    part_real, part_imag = lax.all_to_all(
        jnp.stack([lift_real, lift_imag]), "grp", split_axis=3, concat_axis=2, tiled=True
    )
    real_out = contract("akb,nk->anb", part_real, cos_second) - contract(
        "akb,nk->anb", part_imag, sin_second
    )
    imag_out = contract("akb,nk->anb", part_real, sin_second) + contract(
        "akb,nk->anb", part_imag, cos_second
    )
    first_own = domain_index * first_part + jnp.arange(first_part, dtype=jnp.int32)
    cos_turn, sin_turn = rotation(
        first_own[:, None, None] * (second_freq[None, :, None] * N3 + depth_global[None, None, :]),
        cycle_len,
    )
    spin_real = real_out * cos_turn - imag_out * sin_turn
    spin_imag = real_out * sin_turn + imag_out * cos_turn
    inverse_factor = 1.0 / math.sqrt(cycle_len)
    part_real, part_imag = lax.all_to_all(
        jnp.stack([spin_real, spin_imag]), "dom", split_axis=2, concat_axis=1, tiled=True
    )
    summed = contract("kab,nk->nab", part_real, cos_first) - contract(
        "kab,nk->nab", part_imag, sin_first
    )
    volt_part = summed * inverse_factor
    volt_slab = lax.all_to_all(volt_part, "grp", split_axis=0, concat_axis=2, tiled=True).reshape(
        R1 * own_rows, BINS
    )
    owned_volts = contract("sb,sj->bj", picker, volt_slab)
    volt_rows = dom_sum(owned_volts, domains)
    drifted = energies - 0.5 * jnp.sin(two_pi * (positions - 0.5 * BINS) / BINS)
    positions_out, energies_out = kick_call(positions, drifted, volt_rows)
    return (positions_out, energies_out, spectrum)


def solution(mesh):
    placed = (
        P("grp", "dom"),
        P("grp", "dom"),
        P("grp"),
        P(None, None, "dom", "grp", None),
        P(None, None, "dom", "grp", None),
    )
    return jax.shard_map(
        on_device,
        mesh=mesh,
        in_specs=placed,
        out_specs=(P("grp", "dom"), P("grp", "dom"), P(None, "dom", "grp", None)),
        check_vma=False,
    )
```

```python
import math

import jax
import jax.numpy as jnp
from jax import lax
from jax.sharding import PartitionSpec as P
from jax.experimental import pallas as pl
from jax.experimental.pallas import tpu as pltpu

BINS = 32
N3 = 256
R1 = 8
R2 = 8
HIST = 2
BUNCH_GRP = 704
P_DEV = 256


highest = lax.Precision.HIGHEST
two_pi = 2.0 * math.pi


def kernel_table(places):
    centers = jnp.arange(BINS, dtype=jnp.float32) + 0.5
    offset = places[:, None, :] - centers[None, :, None]
    return jnp.exp(-0.5 * offset * offset)


def dft_tables(length):
    series = jnp.arange(length, dtype=jnp.int32)
    windings = series[:, None] * series[None, :] % length
    angles = windings.astype(jnp.float32) * (two_pi / length)
    return (jnp.cos(angles), jnp.sin(angles))


def rotation(windings, modulus):
    angles = (windings % modulus).astype(jnp.float32) * (two_pi / modulus)
    return (jnp.cos(angles), jnp.sin(angles))


def contract(pattern, operand, matrix):
    return jnp.einsum(pattern, operand, matrix, precision=lax.Precision.HIGH)


def pick(pattern, operand, matrix):
    return jnp.einsum(pattern, operand, matrix, precision=highest)


def dom_sum(rows, domains):
    chunk = rows.shape[0] // domains
    pieces = lax.all_to_all(rows.reshape(domains, chunk, BINS), "dom", 0, 0, tiled=True)
    mine = jnp.sum(pieces, axis=0)
    spread = jnp.broadcast_to(mine[None], (domains, chunk, BINS))
    return lax.all_to_all(spread, "dom", 0, 0, tiled=True).reshape(rows.shape)


KICK_ROWS = 64
SUB_ROWS = 8


def kick_kernel(pos_ref, drift_ref, volt_ref, pos_out, en_out):
    def sub_block(i, carry):
        rows = pl.ds(pl.multiple_of(i * SUB_ROWS, SUB_ROWS), SUB_ROWS)
        place = pos_ref[rows, :]
        volts = volt_ref[rows, :]
        weighted = jnp.zeros_like(place)
        norm = jnp.zeros_like(place)
        for j in range(BINS):
            offset = place - (j + 0.5)
            table = jnp.exp(-0.5 * offset * offset)
            weighted = weighted + table * volts[:, j : j + 1]
            norm = norm + table
        energy = drift_ref[rows, :] - weighted / norm
        en_out[rows, :] = energy
        pos_out[rows, :] = place + 0.25 * energy
        return carry

    lax.fori_loop(0, KICK_ROWS // SUB_ROWS, sub_block, 0)


def kick_call(positions, drifted, volt_rows):
    bunches, width = positions.shape
    wide = pl.BlockSpec((KICK_ROWS, width), lambda i: (i, 0))
    narrow = pl.BlockSpec((KICK_ROWS, BINS), lambda i: (i, 0))
    shape = jax.ShapeDtypeStruct(positions.shape, jnp.float32)
    return pl.pallas_call(
        kick_kernel,
        grid=(bunches // KICK_ROWS,),
        in_specs=[wide, wide, narrow],
        out_specs=[wide, wide],
        out_shape=[shape, shape],
        cost_estimate=pl.CostEstimate(
            flops=12 * bunches * width * BINS,
            transcendentals=bunches * width * BINS,
            bytes_accessed=4 * bunches * (4 * width + BINS),
        ),
    )(positions, drifted, volt_rows)


def on_device(positions, energies, bucket, impedance, history):
    groups = lax.axis_size("grp")
    domains = lax.axis_size("dom")
    group_index = lax.axis_index("grp")
    domain_index = lax.axis_index("dom")
    first_len = R1 * groups
    second_len = R2 * domains
    cycle_len = first_len * second_len * N3
    plane_len = second_len * N3
    depth_len = N3 // groups
    first_part = first_len // domains
    second_part = second_len // groups
    per_row = N3 // BINS
    row_buckets = second_len * per_row
    own_rows = R2 * per_row
    partial_value = jnp.sum(kernel_table(positions), axis=2) / float(P_DEV * domains)
    first_row = bucket // row_buckets
    within = bucket % row_buckets
    owner_dom = within // own_rows
    owned_here = owner_dom == domain_index
    slot = jnp.where(owned_here, first_row * own_rows + within - owner_dom * own_rows, -1)
    picker = (slot[None, :] == jnp.arange(R1 * own_rows, dtype=jnp.int32)[:, None]).astype(jnp.float32)
    totals = dom_sum(partial_value, domains)
    line_slab = pick("sb,bj->sj", picker, totals)
    density = line_slab.reshape(R1, R2, N3)
    cos_first, sin_first = dft_tables(first_len)
    cos_second, sin_second = dft_tables(second_len)
    cos_third, sin_third = dft_tables(N3)
    received = lax.all_to_all(density, "grp", split_axis=2, concat_axis=0, tiled=True)
    real_out = contract("nab,kn->abk", received, cos_first)
    imag_out = -contract("nab,kn->abk", received, sin_first)
    rows_real = real_out
    rows_imag = imag_out
    second_global = domain_index * R2 + jnp.arange(R2, dtype=jnp.int32)
    depth_global = group_index * depth_len + jnp.arange(depth_len, dtype=jnp.int32)
    first_freq = jnp.arange(first_len, dtype=jnp.int32)
    cos_turn, sin_turn = rotation(
        first_freq[None, None, :]
        * (second_global[:, None, None] * N3 + depth_global[None, :, None]),
        cycle_len,
    )
    twist_real = rows_real * cos_turn + rows_imag * sin_turn
    twist_imag = rows_imag * cos_turn - rows_real * sin_turn
    part_real, part_imag = lax.all_to_all(
        jnp.stack([twist_real, twist_imag]), "dom", split_axis=3, concat_axis=1, tiled=True
    )
    real_out = contract("nbk,mn->bkm", part_real, cos_second) + contract(
        "nbk,mn->bkm", part_imag, sin_second
    )
    imag_out = contract("nbk,mn->bkm", part_imag, cos_second) - contract(
        "nbk,mn->bkm", part_real, sin_second
    )
    cols_real = real_out
    cols_imag = imag_out
    second_freq = jnp.arange(second_len, dtype=jnp.int32)
    cos_turn, sin_turn = rotation(
        depth_global[:, None, None] * second_freq[None, None, :], plane_len
    )
    turned_real = cols_real * cos_turn + cols_imag * sin_turn
    turned_imag = cols_imag * cos_turn - cols_real * sin_turn
    part_real, part_imag = lax.all_to_all(
        jnp.stack([turned_real, turned_imag]), "grp", split_axis=3, concat_axis=1, tiled=True
    )
    real_out = contract("nac,kn->ack", part_real, cos_third) + contract(
        "nac,kn->ack", part_imag, sin_third
    )
    imag_out = contract("nac,kn->ack", part_imag, cos_third) - contract(
        "nac,kn->ack", part_real, sin_third
    )
    full_real = real_out
    full_imag = imag_out
    norm_factor = 1.0 / math.sqrt(BUNCH_GRP * groups)
    spec_real = full_real * norm_factor
    spec_imag = full_imag * norm_factor
    spectrum = jnp.stack([spec_real, spec_imag])
    volt_real = impedance[0, 0] * spec_real - impedance[0, 1] * spec_imag
    volt_imag = impedance[0, 0] * spec_imag + impedance[0, 1] * spec_real
    for earlier in range(HIST):
        past_real = history[earlier, 0]
        past_imag = history[earlier, 1]
        volt_real = (
            volt_real
            + impedance[earlier + 1, 0] * past_real
            - impedance[earlier + 1, 1] * past_imag
        )
        volt_imag = (
            volt_imag
            + impedance[earlier + 1, 0] * past_imag
            + impedance[earlier + 1, 1] * past_real
        )
    back_real = contract("ack,nk->acn", volt_real, cos_third) - contract(
        "ack,nk->acn", volt_imag, sin_third
    )
    back_imag = contract("ack,nk->acn", volt_real, sin_third) + contract(
        "ack,nk->acn", volt_imag, cos_third
    )
    second_own = group_index * second_part + jnp.arange(second_part, dtype=jnp.int32)
    depth_all = jnp.arange(N3, dtype=jnp.int32)
    cos_turn, sin_turn = rotation(second_own[None, :, None] * depth_all[None, None, :], plane_len)
    lift_real = back_real * cos_turn - back_imag * sin_turn
    lift_imag = back_real * sin_turn + back_imag * cos_turn
    part_real, part_imag = lax.all_to_all(
        jnp.stack([lift_real, lift_imag]), "grp", split_axis=3, concat_axis=2, tiled=True
    )
    real_out = contract("akb,nk->anb", part_real, cos_second) - contract(
        "akb,nk->anb", part_imag, sin_second
    )
    imag_out = contract("akb,nk->anb", part_real, sin_second) + contract(
        "akb,nk->anb", part_imag, cos_second
    )
    first_own = domain_index * first_part + jnp.arange(first_part, dtype=jnp.int32)
    cos_turn, sin_turn = rotation(
        first_own[:, None, None] * (second_freq[None, :, None] * N3 + depth_global[None, None, :]),
        cycle_len,
    )
    spin_real = real_out * cos_turn - imag_out * sin_turn
    spin_imag = real_out * sin_turn + imag_out * cos_turn
    inverse_factor = 1.0 / math.sqrt(cycle_len)
    part_real, part_imag = lax.all_to_all(
        jnp.stack([spin_real, spin_imag]), "dom", split_axis=2, concat_axis=1, tiled=True
    )
    summed = contract("kab,nk->nab", part_real, cos_first) - contract(
        "kab,nk->nab", part_imag, sin_first
    )
    volt_part = summed * inverse_factor
    volt_slab = lax.all_to_all(volt_part, "grp", split_axis=0, concat_axis=2, tiled=True).reshape(
        R1 * own_rows, BINS
    )
    owned_volts = pick("sb,sj->bj", picker, volt_slab)
    volt_rows = dom_sum(owned_volts, domains)
    drifted = energies - 0.5 * jnp.sin(two_pi * (positions - 0.5 * BINS) / BINS)
    positions_out, energies_out = kick_call(positions, drifted, volt_rows)
    return (positions_out, energies_out, spectrum)


def solution(mesh):
    placed = (
        P("grp", "dom"),
        P("grp", "dom"),
        P("grp"),
        P(None, None, "dom", "grp", None),
        P(None, None, "dom", "grp", None),
    )
    return jax.shard_map(
        on_device,
        mesh=mesh,
        in_specs=placed,
        out_specs=(P("grp", "dom"), P("grp", "dom"), P(None, "dom", "grp", None)),
        check_vma=False,
    )
```

```python
import math

import jax
import jax.numpy as jnp
from jax import lax
from jax.sharding import PartitionSpec as P
from jax.experimental import pallas as pl
from jax.experimental.pallas import tpu as pltpu

BINS = 32
N3 = 256
R1 = 8
R2 = 8
HIST = 2
BUNCH_GRP = 704
P_DEV = 256


highest = lax.Precision.HIGHEST
two_pi = 2.0 * math.pi


def kernel_table(places):
    centers = jnp.arange(BINS, dtype=jnp.float32) + 0.5
    offset = places[:, None, :] - centers[None, :, None]
    return jnp.exp(-0.5 * offset * offset)


def dft_tables(length):
    series = jnp.arange(length, dtype=jnp.int32)
    windings = series[:, None] * series[None, :] % length
    angles = windings.astype(jnp.float32) * (two_pi / length)
    return (jnp.cos(angles), jnp.sin(angles))


def rotation(windings, modulus):
    angles = (windings % modulus).astype(jnp.float32) * (two_pi / modulus)
    return (jnp.cos(angles), jnp.sin(angles))


def contract(pattern, operand, matrix):
    return jnp.einsum(pattern, operand, matrix, precision=highest)


def block_table(length):
    cos_t, sin_t = dft_tables(length)
    return jnp.stack([jnp.stack([cos_t, -sin_t], axis=1), jnp.stack([sin_t, cos_t], axis=1)])


def conjugate(table):
    return table * jnp.array([1.0, -1.0], jnp.float32)[None, None, :, None] * jnp.array(
        [1.0, -1.0], jnp.float32
    )[:, None, None, None]


def turn(pair, cos_t, sin_t):
    return jnp.stack([pair[0] * cos_t - pair[1] * sin_t, pair[0] * sin_t + pair[1] * cos_t])


def dom_sum(rows, domains):
    chunk = rows.shape[0] // domains
    pieces = lax.all_to_all(rows.reshape(domains, chunk, BINS), "dom", 0, 0, tiled=True)
    mine = jnp.sum(pieces, axis=0)
    spread = jnp.broadcast_to(mine[None], (domains, chunk, BINS))
    return lax.all_to_all(spread, "dom", 0, 0, tiled=True).reshape(rows.shape)


KICK_ROWS = 64
SUB_ROWS = 8


def kick_kernel(pos_ref, drift_ref, volt_ref, pos_out, en_out):
    def sub_block(i, carry):
        rows = pl.ds(pl.multiple_of(i * SUB_ROWS, SUB_ROWS), SUB_ROWS)
        place = pos_ref[rows, :]
        volts = volt_ref[rows, :]
        weighted = jnp.zeros_like(place)
        norm = jnp.zeros_like(place)
        for j in range(BINS):
            offset = place - (j + 0.5)
            table = jnp.exp(-0.5 * offset * offset)
            weighted = weighted + table * volts[:, j : j + 1]
            norm = norm + table
        energy = drift_ref[rows, :] - weighted / norm
        en_out[rows, :] = energy
        pos_out[rows, :] = place + 0.25 * energy
        return carry

    lax.fori_loop(0, KICK_ROWS // SUB_ROWS, sub_block, 0)


def kick_call(positions, drifted, volt_rows):
    bunches, width = positions.shape
    wide = pl.BlockSpec((KICK_ROWS, width), lambda i: (i, 0))
    narrow = pl.BlockSpec((KICK_ROWS, BINS), lambda i: (i, 0))
    shape = jax.ShapeDtypeStruct(positions.shape, jnp.float32)
    return pl.pallas_call(
        kick_kernel,
        grid=(bunches // KICK_ROWS,),
        in_specs=[wide, wide, narrow],
        out_specs=[wide, wide],
        out_shape=[shape, shape],
        cost_estimate=pl.CostEstimate(
            flops=12 * bunches * width * BINS,
            transcendentals=bunches * width * BINS,
            bytes_accessed=4 * bunches * (4 * width + BINS),
        ),
    )(positions, drifted, volt_rows)


def on_device(positions, energies, bucket, impedance, history):
    groups = lax.axis_size("grp")
    domains = lax.axis_size("dom")
    group_index = lax.axis_index("grp")
    domain_index = lax.axis_index("dom")
    first_len = R1 * groups
    second_len = R2 * domains
    cycle_len = first_len * second_len * N3
    plane_len = second_len * N3
    depth_len = N3 // groups
    first_part = first_len // domains
    second_part = second_len // groups
    per_row = N3 // BINS
    row_buckets = second_len * per_row
    own_rows = R2 * per_row
    partial_value = jnp.sum(kernel_table(positions), axis=2) / float(P_DEV * domains)
    first_row = bucket // row_buckets
    within = bucket % row_buckets
    owner_dom = within // own_rows
    owned_here = owner_dom == domain_index
    slot = jnp.where(owned_here, first_row * own_rows + within - owner_dom * own_rows, -1)
    picker = (slot[None, :] == jnp.arange(R1 * own_rows, dtype=jnp.int32)[:, None]).astype(jnp.float32)
    totals = dom_sum(partial_value, domains)
    line_slab = contract("sb,bj->sj", picker, totals)
    density = line_slab.reshape(R1, R2, N3)
    first_table = block_table(first_len)
    second_table = block_table(second_len)
    third_table = block_table(N3)
    received = lax.all_to_all(density, "grp", split_axis=2, concat_axis=0, tiled=True)
    rows = contract("nab,nok->oabk", received, first_table[0])
    second_global = domain_index * R2 + jnp.arange(R2, dtype=jnp.int32)
    depth_global = group_index * depth_len + jnp.arange(depth_len, dtype=jnp.int32)
    first_freq = jnp.arange(first_len, dtype=jnp.int32)
    cos_turn, sin_turn = rotation(
        first_freq[None, None, :]
        * (second_global[:, None, None] * N3 + depth_global[None, :, None]),
        cycle_len,
    )
    twist = turn(rows, cos_turn, -sin_turn)
    part = lax.all_to_all(twist, "dom", split_axis=3, concat_axis=1, tiled=True)
    cols = contract("inbk,inom->obkm", part, second_table)
    second_freq = jnp.arange(second_len, dtype=jnp.int32)
    cos_turn, sin_turn = rotation(
        depth_global[:, None, None] * second_freq[None, None, :], plane_len
    )
    turned = turn(cols, cos_turn, -sin_turn)
    part = lax.all_to_all(turned, "grp", split_axis=3, concat_axis=1, tiled=True)
    full = contract("inac,inok->oack", part, third_table)
    norm_factor = 1.0 / math.sqrt(BUNCH_GRP * groups)
    spectrum = full * norm_factor
    spec_real = spectrum[0]
    spec_imag = spectrum[1]
    volt_real = impedance[0, 0] * spec_real - impedance[0, 1] * spec_imag
    volt_imag = impedance[0, 0] * spec_imag + impedance[0, 1] * spec_real
    for earlier in range(HIST):
        past_real = history[earlier, 0]
        past_imag = history[earlier, 1]
        volt_real = (
            volt_real
            + impedance[earlier + 1, 0] * past_real
            - impedance[earlier + 1, 1] * past_imag
        )
        volt_imag = (
            volt_imag
            + impedance[earlier + 1, 0] * past_imag
            + impedance[earlier + 1, 1] * past_real
        )
    back = contract("iack,ikon->oacn", jnp.stack([volt_real, volt_imag]), conjugate(third_table))
    second_own = group_index * second_part + jnp.arange(second_part, dtype=jnp.int32)
    depth_all = jnp.arange(N3, dtype=jnp.int32)
    cos_turn, sin_turn = rotation(second_own[None, :, None] * depth_all[None, None, :], plane_len)
    lift = turn(back, cos_turn, sin_turn)
    part = lax.all_to_all(lift, "grp", split_axis=3, concat_axis=2, tiled=True)
    spun = contract("iakb,ikon->oanb", part, conjugate(second_table))
    first_own = domain_index * first_part + jnp.arange(first_part, dtype=jnp.int32)
    cos_turn, sin_turn = rotation(
        first_own[:, None, None] * (second_freq[None, :, None] * N3 + depth_global[None, None, :]),
        cycle_len,
    )
    spin = turn(spun, cos_turn, sin_turn)
    inverse_factor = 1.0 / math.sqrt(cycle_len)
    part = lax.all_to_all(spin, "dom", split_axis=2, concat_axis=1, tiled=True)
    summed = contract("ikab,ikn->nab", part, conjugate(first_table)[:, :, 0, :])
    volt_part = summed * inverse_factor
    volt_slab = lax.all_to_all(volt_part, "grp", split_axis=0, concat_axis=2, tiled=True).reshape(
        R1 * own_rows, BINS
    )
    owned_volts = contract("sb,sj->bj", picker, volt_slab)
    volt_rows = dom_sum(owned_volts, domains)
    drifted = energies - 0.5 * jnp.sin(two_pi * (positions - 0.5 * BINS) / BINS)
    positions_out, energies_out = kick_call(positions, drifted, volt_rows)
    return (positions_out, energies_out, spectrum)


def solution(mesh):
    placed = (
        P("grp", "dom"),
        P("grp", "dom"),
        P("grp"),
        P(None, None, "dom", "grp", None),
        P(None, None, "dom", "grp", None),
    )
    return jax.shard_map(
        on_device,
        mesh=mesh,
        in_specs=placed,
        out_specs=(P("grp", "dom"), P("grp", "dom"), P(None, "dom", "grp", None)),
        check_vma=False,
    )
```

```python
import math

import jax
import jax.numpy as jnp
from jax import lax
from jax.sharding import PartitionSpec as P
from jax.experimental import pallas as pl
from jax.experimental.pallas import tpu as pltpu

BINS = 32
N3 = 256
R1 = 8
R2 = 8
HIST = 2
BUNCH_GRP = 704
P_DEV = 256


highest = lax.Precision.HIGHEST
two_pi = 2.0 * math.pi


def kernel_table(places):
    centers = jnp.arange(BINS, dtype=jnp.float32) + 0.5
    offset = places[:, None, :] - centers[None, :, None]
    return jnp.exp(-0.5 * offset * offset)


def dft_tables(length):
    series = jnp.arange(length, dtype=jnp.int32)
    windings = series[:, None] * series[None, :] % length
    angles = windings.astype(jnp.float32) * (two_pi / length)
    return (jnp.cos(angles), jnp.sin(angles))


def rotation(windings, modulus):
    angles = (windings % modulus).astype(jnp.float32) * (two_pi / modulus)
    return (jnp.cos(angles), jnp.sin(angles))


def contract(pattern, operand, matrix):
    return jnp.einsum(pattern, operand, matrix, precision=highest)


def block_table(length):
    cos_t, sin_t = dft_tables(length)
    return jnp.stack([jnp.stack([cos_t, -sin_t], axis=1), jnp.stack([sin_t, cos_t], axis=1)])


def conjugate(table):
    return table * jnp.array([1.0, -1.0], jnp.float32)[None, None, :, None] * jnp.array(
        [1.0, -1.0], jnp.float32
    )[:, None, None, None]


def turn(pair, cos_t, sin_t):
    return jnp.stack([pair[0] * cos_t - pair[1] * sin_t, pair[0] * sin_t + pair[1] * cos_t])


def exchange(x, axis_name, split_axis, concat_axis):
    count = lax.axis_size(axis_name)
    front = jnp.moveaxis(x, split_axis, 0)
    rest = front.shape[1:]
    piece = (front.shape[0] // count,) + rest
    sent = front.reshape(count, -1, 128)
    got = lax.all_to_all(sent, axis_name, 0, 0, tiled=True).reshape((count,) + piece)
    got = jnp.moveaxis(got, 1, split_axis + 1)
    got = jnp.moveaxis(got, 0, concat_axis)
    shape = list(x.shape)
    shape[split_axis] //= count
    shape[concat_axis] *= count
    return got.reshape(shape)


def dom_sum(rows, domains):
    chunk = rows.shape[0] // domains
    pieces = lax.all_to_all(rows.reshape(domains, chunk, BINS), "dom", 0, 0, tiled=True)
    mine = jnp.sum(pieces, axis=0)
    spread = jnp.broadcast_to(mine[None], (domains, chunk, BINS))
    return lax.all_to_all(spread, "dom", 0, 0, tiled=True).reshape(rows.shape)


KICK_ROWS = 64
SUB_ROWS = 8


def kick_kernel(pos_ref, drift_ref, volt_ref, pos_out, en_out):
    def sub_block(i, carry):
        rows = pl.ds(pl.multiple_of(i * SUB_ROWS, SUB_ROWS), SUB_ROWS)
        place = pos_ref[rows, :]
        volts = volt_ref[rows, :]
        weighted = jnp.zeros_like(place)
        norm = jnp.zeros_like(place)
        for j in range(BINS):
            offset = place - (j + 0.5)
            table = jnp.exp(-0.5 * offset * offset)
            weighted = weighted + table * volts[:, j : j + 1]
            norm = norm + table
        energy = drift_ref[rows, :] - weighted / norm
        en_out[rows, :] = energy
        pos_out[rows, :] = place + 0.25 * energy
        return carry

    lax.fori_loop(0, KICK_ROWS // SUB_ROWS, sub_block, 0)


def kick_call(positions, drifted, volt_rows):
    bunches, width = positions.shape
    wide = pl.BlockSpec((KICK_ROWS, width), lambda i: (i, 0))
    narrow = pl.BlockSpec((KICK_ROWS, BINS), lambda i: (i, 0))
    shape = jax.ShapeDtypeStruct(positions.shape, jnp.float32)
    return pl.pallas_call(
        kick_kernel,
        grid=(bunches // KICK_ROWS,),
        in_specs=[wide, wide, narrow],
        out_specs=[wide, wide],
        out_shape=[shape, shape],
        cost_estimate=pl.CostEstimate(
            flops=12 * bunches * width * BINS,
            transcendentals=bunches * width * BINS,
            bytes_accessed=4 * bunches * (4 * width + BINS),
        ),
    )(positions, drifted, volt_rows)


def on_device(positions, energies, bucket, impedance, history):
    groups = lax.axis_size("grp")
    domains = lax.axis_size("dom")
    group_index = lax.axis_index("grp")
    domain_index = lax.axis_index("dom")
    first_len = R1 * groups
    second_len = R2 * domains
    cycle_len = first_len * second_len * N3
    plane_len = second_len * N3
    depth_len = N3 // groups
    first_part = first_len // domains
    second_part = second_len // groups
    per_row = N3 // BINS
    row_buckets = second_len * per_row
    own_rows = R2 * per_row
    partial_value = jnp.sum(kernel_table(positions), axis=2) / float(P_DEV * domains)
    first_row = bucket // row_buckets
    within = bucket % row_buckets
    owner_dom = within // own_rows
    owned_here = owner_dom == domain_index
    slot = jnp.where(owned_here, first_row * own_rows + within - owner_dom * own_rows, -1)
    picker = (slot[None, :] == jnp.arange(R1 * own_rows, dtype=jnp.int32)[:, None]).astype(jnp.float32)
    totals = dom_sum(partial_value, domains)
    line_slab = contract("sb,bj->sj", picker, totals)
    density = line_slab.reshape(R1, R2, N3)
    first_table = block_table(first_len)
    second_table = block_table(second_len)
    third_table = block_table(N3)
    received = exchange(density, "grp", 2, 0)
    rows = contract("nab,nok->oabk", received, first_table[0])
    second_global = domain_index * R2 + jnp.arange(R2, dtype=jnp.int32)
    depth_global = group_index * depth_len + jnp.arange(depth_len, dtype=jnp.int32)
    first_freq = jnp.arange(first_len, dtype=jnp.int32)
    cos_turn, sin_turn = rotation(
        first_freq[None, None, :]
        * (second_global[:, None, None] * N3 + depth_global[None, :, None]),
        cycle_len,
    )
    twist = turn(rows, cos_turn, -sin_turn)
    part = exchange(twist, "dom", 3, 1)
    cols = contract("inbk,inom->obkm", part, second_table)
    second_freq = jnp.arange(second_len, dtype=jnp.int32)
    cos_turn, sin_turn = rotation(
        depth_global[:, None, None] * second_freq[None, None, :], plane_len
    )
    turned = turn(cols, cos_turn, -sin_turn)
    part = exchange(turned, "grp", 3, 1)
    full = contract("inac,inok->oack", part, third_table)
    norm_factor = 1.0 / math.sqrt(BUNCH_GRP * groups)
    spectrum = full * norm_factor
    spec_real = spectrum[0]
    spec_imag = spectrum[1]
    volt_real = impedance[0, 0] * spec_real - impedance[0, 1] * spec_imag
    volt_imag = impedance[0, 0] * spec_imag + impedance[0, 1] * spec_real
    for earlier in range(HIST):
        past_real = history[earlier, 0]
        past_imag = history[earlier, 1]
        volt_real = (
            volt_real
            + impedance[earlier + 1, 0] * past_real
            - impedance[earlier + 1, 1] * past_imag
        )
        volt_imag = (
            volt_imag
            + impedance[earlier + 1, 0] * past_imag
            + impedance[earlier + 1, 1] * past_real
        )
    back = contract("iack,ikon->oacn", jnp.stack([volt_real, volt_imag]), conjugate(third_table))
    second_own = group_index * second_part + jnp.arange(second_part, dtype=jnp.int32)
    depth_all = jnp.arange(N3, dtype=jnp.int32)
    cos_turn, sin_turn = rotation(second_own[None, :, None] * depth_all[None, None, :], plane_len)
    lift = turn(back, cos_turn, sin_turn)
    part = exchange(lift, "grp", 3, 2)
    spun = contract("iakb,ikon->oanb", part, conjugate(second_table))
    first_own = domain_index * first_part + jnp.arange(first_part, dtype=jnp.int32)
    cos_turn, sin_turn = rotation(
        first_own[:, None, None] * (second_freq[None, :, None] * N3 + depth_global[None, None, :]),
        cycle_len,
    )
    spin = turn(spun, cos_turn, sin_turn)
    inverse_factor = 1.0 / math.sqrt(cycle_len)
    part = exchange(spin, "dom", 2, 1)
    summed = contract("ikab,ikn->nab", part, conjugate(first_table)[:, :, 0, :])
    volt_part = summed * inverse_factor
    volt_slab = exchange(volt_part, "grp", 0, 2).reshape(
        R1 * own_rows, BINS
    )
    owned_volts = contract("sb,sj->bj", picker, volt_slab)
    volt_rows = dom_sum(owned_volts, domains)
    drifted = energies - 0.5 * jnp.sin(two_pi * (positions - 0.5 * BINS) / BINS)
    positions_out, energies_out = kick_call(positions, drifted, volt_rows)
    return (positions_out, energies_out, spectrum)


def solution(mesh):
    placed = (
        P("grp", "dom"),
        P("grp", "dom"),
        P("grp"),
        P(None, None, "dom", "grp", None),
        P(None, None, "dom", "grp", None),
    )
    return jax.shard_map(
        on_device,
        mesh=mesh,
        in_specs=placed,
        out_specs=(P("grp", "dom"), P("grp", "dom"), P(None, "dom", "grp", None)),
        check_vma=False,
    )
```

```python
import math

import jax
import jax.numpy as jnp
from jax import lax
from jax.sharding import PartitionSpec as P
from jax.experimental import pallas as pl
from jax.experimental.pallas import tpu as pltpu

BINS = 32
N3 = 256
R1 = 8
R2 = 8
HIST = 2
BUNCH_GRP = 704
P_DEV = 256


highest = lax.Precision.HIGHEST
two_pi = 2.0 * math.pi


def kernel_table(places):
    centers = jnp.arange(BINS, dtype=jnp.float32) + 0.5
    offset = places[:, None, :] - centers[None, :, None]
    return jnp.exp(-0.5 * offset * offset)


def dft_tables(length):
    series = jnp.arange(length, dtype=jnp.int32)
    windings = series[:, None] * series[None, :] % length
    angles = windings.astype(jnp.float32) * (two_pi / length)
    return (jnp.cos(angles), jnp.sin(angles))


def rotation(windings, modulus):
    angles = (windings % modulus).astype(jnp.float32) * (two_pi / modulus)
    return (jnp.cos(angles), jnp.sin(angles))


def contract(pattern, operand, matrix):
    return jnp.einsum(pattern, operand, matrix, precision=highest)


def block_table(length):
    cos_t, sin_t = dft_tables(length)
    return jnp.stack([jnp.stack([cos_t, -sin_t], axis=1), jnp.stack([sin_t, cos_t], axis=1)])


def conjugate(table):
    return table * jnp.array([1.0, -1.0], jnp.float32)[None, None, :, None] * jnp.array(
        [1.0, -1.0], jnp.float32
    )[:, None, None, None]


def turn(pair, cos_t, sin_t):
    return jnp.stack([pair[0] * cos_t - pair[1] * sin_t, pair[0] * sin_t + pair[1] * cos_t])


def exchange(x, axis_name, split_axis, concat_axis):
    count = lax.axis_size(axis_name)
    front = jnp.moveaxis(x, split_axis, 0)
    rest = front.shape[1:]
    piece = (front.shape[0] // count,) + rest
    sent = front.reshape(count, -1, 128)
    got = lax.all_to_all(sent, axis_name, 0, 0, tiled=True).reshape((count,) + piece)
    got = jnp.moveaxis(got, 1, split_axis + 1)
    got = jnp.moveaxis(got, 0, concat_axis)
    shape = list(x.shape)
    shape[split_axis] //= count
    shape[concat_axis] *= count
    return got.reshape(shape)


def dom_sum(rows, domains):
    chunk = rows.shape[0] // domains
    pieces = lax.all_to_all(rows.reshape(domains, -1, 128), "dom", 0, 0, tiled=True)
    mine = jnp.sum(pieces, axis=0)
    spread = jnp.broadcast_to(mine[None], (domains,) + mine.shape)
    return lax.all_to_all(spread, "dom", 0, 0, tiled=True).reshape(rows.shape)


KICK_ROWS = 64
SUB_ROWS = 8


def kick_kernel(pos_ref, drift_ref, volt_ref, pos_out, en_out):
    def sub_block(i, carry):
        rows = pl.ds(pl.multiple_of(i * SUB_ROWS, SUB_ROWS), SUB_ROWS)
        place = pos_ref[rows, :]
        volts = volt_ref[rows, :]
        weighted = jnp.zeros_like(place)
        norm = jnp.zeros_like(place)
        for j in range(BINS):
            offset = place - (j + 0.5)
            table = jnp.exp(-0.5 * offset * offset)
            weighted = weighted + table * volts[:, j : j + 1]
            norm = norm + table
        energy = drift_ref[rows, :] - weighted / norm
        en_out[rows, :] = energy
        pos_out[rows, :] = place + 0.25 * energy
        return carry

    lax.fori_loop(0, KICK_ROWS // SUB_ROWS, sub_block, 0)


def kick_call(positions, drifted, volt_rows):
    bunches, width = positions.shape
    wide = pl.BlockSpec((KICK_ROWS, width), lambda i: (i, 0))
    narrow = pl.BlockSpec((KICK_ROWS, BINS), lambda i: (i, 0))
    shape = jax.ShapeDtypeStruct(positions.shape, jnp.float32)
    return pl.pallas_call(
        kick_kernel,
        grid=(bunches // KICK_ROWS,),
        in_specs=[wide, wide, narrow],
        out_specs=[wide, wide],
        out_shape=[shape, shape],
        cost_estimate=pl.CostEstimate(
            flops=12 * bunches * width * BINS,
            transcendentals=bunches * width * BINS,
            bytes_accessed=4 * bunches * (4 * width + BINS),
        ),
    )(positions, drifted, volt_rows)


def on_device(positions, energies, bucket, impedance, history):
    groups = lax.axis_size("grp")
    domains = lax.axis_size("dom")
    group_index = lax.axis_index("grp")
    domain_index = lax.axis_index("dom")
    first_len = R1 * groups
    second_len = R2 * domains
    cycle_len = first_len * second_len * N3
    plane_len = second_len * N3
    depth_len = N3 // groups
    first_part = first_len // domains
    second_part = second_len // groups
    per_row = N3 // BINS
    row_buckets = second_len * per_row
    own_rows = R2 * per_row
    partial_value = jnp.sum(kernel_table(positions), axis=2) / float(P_DEV * domains)
    first_row = bucket // row_buckets
    within = bucket % row_buckets
    owner_dom = within // own_rows
    owned_here = owner_dom == domain_index
    slot = jnp.where(owned_here, first_row * own_rows + within - owner_dom * own_rows, -1)
    picker = (slot[None, :] == jnp.arange(R1 * own_rows, dtype=jnp.int32)[:, None]).astype(jnp.float32)
    totals = dom_sum(partial_value, domains)
    line_slab = contract("sb,bj->sj", picker, totals)
    density = line_slab.reshape(R1, R2, N3)
    first_table = block_table(first_len)
    second_table = block_table(second_len)
    third_table = block_table(N3)
    received = exchange(density, "grp", 2, 0)
    rows = contract("nab,nok->oabk", received, first_table[0])
    second_global = domain_index * R2 + jnp.arange(R2, dtype=jnp.int32)
    depth_global = group_index * depth_len + jnp.arange(depth_len, dtype=jnp.int32)
    first_freq = jnp.arange(first_len, dtype=jnp.int32)
    cos_turn, sin_turn = rotation(
        first_freq[None, None, :]
        * (second_global[:, None, None] * N3 + depth_global[None, :, None]),
        cycle_len,
    )
    twist = turn(rows, cos_turn, -sin_turn)
    part = exchange(twist, "dom", 3, 1)
    cols = contract("inbk,inom->obkm", part, second_table)
    second_freq = jnp.arange(second_len, dtype=jnp.int32)
    cos_turn, sin_turn = rotation(
        depth_global[:, None, None] * second_freq[None, None, :], plane_len
    )
    turned = turn(cols, cos_turn, -sin_turn)
    part = exchange(turned, "grp", 3, 1)
    full = contract("inac,inok->oack", part, third_table)
    norm_factor = 1.0 / math.sqrt(BUNCH_GRP * groups)
    spectrum = full * norm_factor
    spec_real = spectrum[0]
    spec_imag = spectrum[1]
    volt_real = impedance[0, 0] * spec_real - impedance[0, 1] * spec_imag
    volt_imag = impedance[0, 0] * spec_imag + impedance[0, 1] * spec_real
    for earlier in range(HIST):
        past_real = history[earlier, 0]
        past_imag = history[earlier, 1]
        volt_real = (
            volt_real
            + impedance[earlier + 1, 0] * past_real
            - impedance[earlier + 1, 1] * past_imag
        )
        volt_imag = (
            volt_imag
            + impedance[earlier + 1, 0] * past_imag
            + impedance[earlier + 1, 1] * past_real
        )
    back = contract("iack,ikon->oacn", jnp.stack([volt_real, volt_imag]), conjugate(third_table))
    second_own = group_index * second_part + jnp.arange(second_part, dtype=jnp.int32)
    depth_all = jnp.arange(N3, dtype=jnp.int32)
    cos_turn, sin_turn = rotation(second_own[None, :, None] * depth_all[None, None, :], plane_len)
    lift = turn(back, cos_turn, sin_turn)
    part = exchange(lift, "grp", 3, 2)
    spun = contract("iakb,ikon->oanb", part, conjugate(second_table))
    first_own = domain_index * first_part + jnp.arange(first_part, dtype=jnp.int32)
    cos_turn, sin_turn = rotation(
        first_own[:, None, None] * (second_freq[None, :, None] * N3 + depth_global[None, None, :]),
        cycle_len,
    )
    spin = turn(spun, cos_turn, sin_turn)
    inverse_factor = 1.0 / math.sqrt(cycle_len)
    part = exchange(spin, "dom", 2, 1)
    summed = contract("ikab,ikn->nab", part, conjugate(first_table)[:, :, 0, :])
    volt_part = summed * inverse_factor
    volt_slab = exchange(volt_part, "grp", 0, 2).reshape(
        R1 * own_rows, BINS
    )
    owned_volts = contract("sb,sj->bj", picker, volt_slab)
    volt_rows = dom_sum(owned_volts, domains)
    drifted = energies - 0.5 * jnp.sin(two_pi * (positions - 0.5 * BINS) / BINS)
    positions_out, energies_out = kick_call(positions, drifted, volt_rows)
    return (positions_out, energies_out, spectrum)


def solution(mesh):
    placed = (
        P("grp", "dom"),
        P("grp", "dom"),
        P("grp"),
        P(None, None, "dom", "grp", None),
        P(None, None, "dom", "grp", None),
    )
    return jax.shard_map(
        on_device,
        mesh=mesh,
        in_specs=placed,
        out_specs=(P("grp", "dom"), P("grp", "dom"), P(None, "dom", "grp", None)),
        check_vma=False,
    )
```

```python
import math

import jax
import jax.numpy as jnp
from jax import lax
from jax.sharding import PartitionSpec as P
from jax.experimental import pallas as pl
from jax.experimental.pallas import tpu as pltpu

BINS = 32
N3 = 256
R1 = 8
R2 = 8
HIST = 2
BUNCH_GRP = 704
P_DEV = 256


highest = lax.Precision.HIGHEST
two_pi = 2.0 * math.pi


def kernel_table(places):
    centers = jnp.arange(BINS, dtype=jnp.float32) + 0.5
    offset = places[:, None, :] - centers[None, :, None]
    return jnp.exp(-0.5 * offset * offset)


def dft_tables(length):
    series = jnp.arange(length, dtype=jnp.int32)
    windings = series[:, None] * series[None, :] % length
    angles = windings.astype(jnp.float32) * (two_pi / length)
    return (jnp.cos(angles), jnp.sin(angles))


def rotation(windings, modulus):
    angles = (windings % modulus).astype(jnp.float32) * (two_pi / modulus)
    return (jnp.cos(angles), jnp.sin(angles))


def contract(pattern, operand, matrix):
    return jnp.einsum(pattern, operand, matrix, precision=highest)


def block_table(length):
    cos_t, sin_t = dft_tables(length)
    return jnp.stack([jnp.stack([cos_t, -sin_t], axis=1), jnp.stack([sin_t, cos_t], axis=1)])


def conjugate(table):
    return table * jnp.array([1.0, -1.0], jnp.float32)[None, None, :, None] * jnp.array(
        [1.0, -1.0], jnp.float32
    )[:, None, None, None]


def turn(pair, cos_t, sin_t):
    return jnp.stack([pair[0] * cos_t - pair[1] * sin_t, pair[0] * sin_t + pair[1] * cos_t])


def exchange(x, axis_name, split_axis, concat_axis):
    count = lax.axis_size(axis_name)
    front = jnp.moveaxis(x, split_axis, 0)
    rest = front.shape[1:]
    piece = (front.shape[0] // count,) + rest
    sent = front.reshape(count, -1, 128)
    got = lax.all_to_all(sent, axis_name, 0, 0, tiled=True).reshape((count,) + piece)
    got = jnp.moveaxis(got, 1, split_axis + 1)
    got = jnp.moveaxis(got, 0, concat_axis)
    shape = list(x.shape)
    shape[split_axis] //= count
    shape[concat_axis] *= count
    return got.reshape(shape)


def dom_sum(rows, domains):
    chunk = rows.shape[0] // domains
    pieces = lax.all_to_all(rows.reshape(domains, -1, 128), "dom", 0, 0, tiled=True)
    mine = jnp.sum(pieces, axis=0)
    spread = jnp.broadcast_to(mine[None], (domains,) + mine.shape)
    return lax.all_to_all(spread, "dom", 0, 0, tiled=True).reshape(rows.shape)


KICK_ROWS = 88
SUB_ROWS = 8
CHUNKS = 4


def weight_kernel(pos_ref, out_ref):
    def sub_block(i, carry):
        rows = pl.ds(pl.multiple_of(i * SUB_ROWS, SUB_ROWS), SUB_ROWS)
        place = pos_ref[rows, :]
        norm = jnp.zeros_like(place)
        for j in range(BINS):
            offset = place - (j + 0.5)
            table = jnp.exp(-0.5 * offset * offset)
            out_ref[rows, j, :] = table
            norm = norm + table
        scale = 1.0 / norm
        for j in range(BINS):
            out_ref[rows, j, :] = out_ref[rows, j, :] * scale
        return carry

    lax.fori_loop(0, KICK_ROWS // SUB_ROWS, sub_block, 0)


def weight_call(positions):
    bunches, width = positions.shape
    return pl.pallas_call(
        weight_kernel,
        grid=(bunches // KICK_ROWS,),
        in_specs=[pl.BlockSpec((KICK_ROWS, width), lambda i: (i, 0))],
        out_specs=pl.BlockSpec((KICK_ROWS, BINS, width), lambda i: (i, 0, 0)),
        out_shape=jax.ShapeDtypeStruct((bunches, BINS, width), jnp.float32),
        cost_estimate=pl.CostEstimate(
            flops=10 * bunches * width * BINS,
            transcendentals=bunches * width * BINS,
            bytes_accessed=4 * bunches * width * (BINS + 1),
        ),
    )(positions)


def kick_kernel(pos_ref, drift_ref, volt_ref, weight_ref, pos_out, en_out):
    def sub_block(i, carry):
        rows = pl.ds(pl.multiple_of(i * SUB_ROWS, SUB_ROWS), SUB_ROWS)
        volts = volt_ref[rows, :]
        kick = weight_ref[rows, 0, :] * volts[:, 0:1]
        for j in range(1, BINS):
            kick = kick + weight_ref[rows, j, :] * volts[:, j : j + 1]
        energy = drift_ref[rows, :] - kick
        en_out[rows, :] = energy
        pos_out[rows, :] = pos_ref[rows, :] + 0.25 * energy
        return carry

    lax.fori_loop(0, KICK_ROWS // SUB_ROWS, sub_block, 0)


def kick_call(positions, drifted, volt_rows, weights):
    bunches, width = positions.shape
    wide = pl.BlockSpec((KICK_ROWS, width), lambda i: (i, 0))
    narrow = pl.BlockSpec((KICK_ROWS, BINS), lambda i: (i, 0))
    table = pl.BlockSpec((KICK_ROWS, BINS, width), lambda i: (i, 0, 0))
    shape = jax.ShapeDtypeStruct(positions.shape, jnp.float32)
    return pl.pallas_call(
        kick_kernel,
        grid=(bunches // KICK_ROWS,),
        in_specs=[wide, wide, narrow, table],
        out_specs=[wide, wide],
        out_shape=[shape, shape],
        cost_estimate=pl.CostEstimate(
            flops=2 * bunches * width * BINS,
            transcendentals=0,
            bytes_accessed=4 * bunches * (width * (BINS + 4) + BINS),
        ),
    )(positions, drifted, volt_rows, weights)


def on_device(positions, energies, bucket, impedance, history):
    groups = lax.axis_size("grp")
    domains = lax.axis_size("dom")
    group_index = lax.axis_index("grp")
    domain_index = lax.axis_index("dom")
    first_len = R1 * groups
    second_len = R2 * domains
    cycle_len = first_len * second_len * N3
    plane_len = second_len * N3
    depth_len = N3 // groups
    first_part = first_len // domains
    second_part = second_len // groups
    per_row = N3 // BINS
    row_buckets = second_len * per_row
    own_rows = R2 * per_row
    partial_value = jnp.sum(kernel_table(positions), axis=2) / float(P_DEV * domains)
    span = BUNCH_GRP // CHUNKS
    pieces = [slice(c * span, (c + 1) * span) for c in range(CHUNKS)]
    weights = []

    def covered(operand, axis_name, split_axis, concat_axis):
        piece = pieces[len(weights)]
        place, operand = lax.optimization_barrier((positions[piece], operand))
        got = exchange(operand, axis_name, split_axis, concat_axis)
        got, weight = lax.optimization_barrier((got, weight_call(place)))
        weights.append(weight)
        return got
    first_row = bucket // row_buckets
    within = bucket % row_buckets
    owner_dom = within // own_rows
    owned_here = owner_dom == domain_index
    slot = jnp.where(owned_here, first_row * own_rows + within - owner_dom * own_rows, -1)
    picker = (slot[None, :] == jnp.arange(R1 * own_rows, dtype=jnp.int32)[:, None]).astype(jnp.float32)
    totals = dom_sum(partial_value, domains)
    line_slab = contract("sb,bj->sj", picker, totals)
    density = line_slab.reshape(R1, R2, N3)
    first_table = block_table(first_len)
    second_table = block_table(second_len)
    third_table = block_table(N3)
    received = covered(density, "grp", 2, 0)
    rows = contract("nab,nok->oabk", received, first_table[0])
    second_global = domain_index * R2 + jnp.arange(R2, dtype=jnp.int32)
    depth_global = group_index * depth_len + jnp.arange(depth_len, dtype=jnp.int32)
    first_freq = jnp.arange(first_len, dtype=jnp.int32)
    cos_turn, sin_turn = rotation(
        first_freq[None, None, :]
        * (second_global[:, None, None] * N3 + depth_global[None, :, None]),
        cycle_len,
    )
    twist = turn(rows, cos_turn, -sin_turn)
    part = covered(twist, "dom", 3, 1)
    cols = contract("inbk,inom->obkm", part, second_table)
    second_freq = jnp.arange(second_len, dtype=jnp.int32)
    cos_turn, sin_turn = rotation(
        depth_global[:, None, None] * second_freq[None, None, :], plane_len
    )
    turned = turn(cols, cos_turn, -sin_turn)
    part = covered(turned, "grp", 3, 1)
    full = contract("inac,inok->oack", part, third_table)
    norm_factor = 1.0 / math.sqrt(BUNCH_GRP * groups)
    spectrum = full * norm_factor
    spec_real = spectrum[0]
    spec_imag = spectrum[1]
    volt_real = impedance[0, 0] * spec_real - impedance[0, 1] * spec_imag
    volt_imag = impedance[0, 0] * spec_imag + impedance[0, 1] * spec_real
    for earlier in range(HIST):
        past_real = history[earlier, 0]
        past_imag = history[earlier, 1]
        volt_real = (
            volt_real
            + impedance[earlier + 1, 0] * past_real
            - impedance[earlier + 1, 1] * past_imag
        )
        volt_imag = (
            volt_imag
            + impedance[earlier + 1, 0] * past_imag
            + impedance[earlier + 1, 1] * past_real
        )
    back = contract("iack,ikon->oacn", jnp.stack([volt_real, volt_imag]), conjugate(third_table))
    second_own = group_index * second_part + jnp.arange(second_part, dtype=jnp.int32)
    depth_all = jnp.arange(N3, dtype=jnp.int32)
    cos_turn, sin_turn = rotation(second_own[None, :, None] * depth_all[None, None, :], plane_len)
    lift = turn(back, cos_turn, sin_turn)
    part = covered(lift, "grp", 3, 2)
    spun = contract("iakb,ikon->oanb", part, conjugate(second_table))
    first_own = domain_index * first_part + jnp.arange(first_part, dtype=jnp.int32)
    cos_turn, sin_turn = rotation(
        first_own[:, None, None] * (second_freq[None, :, None] * N3 + depth_global[None, None, :]),
        cycle_len,
    )
    spin = turn(spun, cos_turn, sin_turn)
    inverse_factor = 1.0 / math.sqrt(cycle_len)
    part = exchange(spin, "dom", 2, 1)
    summed = contract("ikab,ikn->nab", part, conjugate(first_table)[:, :, 0, :])
    volt_part = summed * inverse_factor
    volt_slab = exchange(volt_part, "grp", 0, 2).reshape(
        R1 * own_rows, BINS
    )
    owned_volts = contract("sb,sj->bj", picker, volt_slab)
    volt_rows = dom_sum(owned_volts, domains)
    drifted = energies - 0.5 * jnp.sin(two_pi * (positions - 0.5 * BINS) / BINS)
    outs = [
        kick_call(positions[piece], drifted[piece], volt_rows[piece], weights[c])
        for c, piece in enumerate(pieces)
    ]
    positions_out = jnp.concatenate([o[0] for o in outs])
    energies_out = jnp.concatenate([o[1] for o in outs])
    return (positions_out, energies_out, spectrum)


def solution(mesh):
    placed = (
        P("grp", "dom"),
        P("grp", "dom"),
        P("grp"),
        P(None, None, "dom", "grp", None),
        P(None, None, "dom", "grp", None),
    )
    return jax.shard_map(
        on_device,
        mesh=mesh,
        in_specs=placed,
        out_specs=(P("grp", "dom"), P("grp", "dom"), P(None, "dom", "grp", None)),
        check_vma=False,
    )
```

```python
import math

import jax
import jax.numpy as jnp
from jax import lax
from jax.sharding import PartitionSpec as P
from jax.experimental import pallas as pl
from jax.experimental.pallas import tpu as pltpu

BINS = 32
N3 = 256
R1 = 8
R2 = 8
HIST = 2
BUNCH_GRP = 704
P_DEV = 256


highest = lax.Precision.HIGHEST
two_pi = 2.0 * math.pi


def kernel_table(places):
    centers = jnp.arange(BINS, dtype=jnp.float32) + 0.5
    offset = places[:, None, :] - centers[None, :, None]
    return jnp.exp(-0.5 * offset * offset)


def dft_tables(length):
    series = jnp.arange(length, dtype=jnp.int32)
    windings = series[:, None] * series[None, :] % length
    angles = windings.astype(jnp.float32) * (two_pi / length)
    return (jnp.cos(angles), jnp.sin(angles))


def rotation(windings, modulus):
    angles = (windings % modulus).astype(jnp.float32) * (two_pi / modulus)
    return (jnp.cos(angles), jnp.sin(angles))


def contract(pattern, operand, matrix):
    return jnp.einsum(pattern, operand, matrix, precision=highest)


def block_table(length):
    cos_t, sin_t = dft_tables(length)
    return jnp.stack([jnp.stack([cos_t, -sin_t], axis=1), jnp.stack([sin_t, cos_t], axis=1)])


def conjugate(table):
    return table * jnp.array([1.0, -1.0], jnp.float32)[None, None, :, None] * jnp.array(
        [1.0, -1.0], jnp.float32
    )[:, None, None, None]


def turn(pair, cos_t, sin_t):
    return jnp.stack([pair[0] * cos_t - pair[1] * sin_t, pair[0] * sin_t + pair[1] * cos_t])


def exchange(x, axis_name, split_axis, concat_axis):
    count = lax.axis_size(axis_name)
    front = jnp.moveaxis(x, split_axis, 0)
    rest = front.shape[1:]
    piece = (front.shape[0] // count,) + rest
    sent = front.reshape(count, -1, 128)
    got = lax.all_to_all(sent, axis_name, 0, 0, tiled=True).reshape((count,) + piece)
    got = jnp.moveaxis(got, 1, split_axis + 1)
    got = jnp.moveaxis(got, 0, concat_axis)
    shape = list(x.shape)
    shape[split_axis] //= count
    shape[concat_axis] *= count
    return got.reshape(shape)


def dom_sum(rows, domains):
    chunk = rows.shape[0] // domains
    pieces = lax.all_to_all(rows.reshape(domains, -1, 128), "dom", 0, 0, tiled=True)
    mine = jnp.sum(pieces, axis=0)
    spread = jnp.broadcast_to(mine[None], (domains,) + mine.shape)
    return lax.all_to_all(spread, "dom", 0, 0, tiled=True).reshape(rows.shape)


KICK_ROWS = 88
SUB_ROWS = 8
CHUNKS = 4


def weight_kernel(pos_ref, table_ref, norm_ref):
    def sub_block(i, carry):
        rows = pl.ds(pl.multiple_of(i * SUB_ROWS, SUB_ROWS), SUB_ROWS)
        place = pos_ref[rows, :]
        norm = jnp.zeros_like(place)
        for j in range(BINS):
            offset = place - (j + 0.5)
            table = jnp.exp(-0.5 * offset * offset)
            table_ref[j, rows, :] = table
            norm = norm + table
        norm_ref[rows, :] = norm
        return carry

    lax.fori_loop(0, KICK_ROWS // SUB_ROWS, sub_block, 0)


def weight_call(positions):
    bunches, width = positions.shape
    wide = pl.BlockSpec((KICK_ROWS, width), lambda i: (i, 0))
    return pl.pallas_call(
        weight_kernel,
        grid=(bunches // KICK_ROWS,),
        in_specs=[wide],
        out_specs=[pl.BlockSpec((BINS, KICK_ROWS, width), lambda i: (0, i, 0)), wide],
        out_shape=[
            jax.ShapeDtypeStruct((BINS, bunches, width), jnp.float32),
            jax.ShapeDtypeStruct((bunches, width), jnp.float32),
        ],
        cost_estimate=pl.CostEstimate(
            flops=6 * bunches * width * BINS,
            transcendentals=bunches * width * BINS,
            bytes_accessed=4 * bunches * width * (BINS + 2),
        ),
    )(positions)


def kick_kernel(pos_ref, drift_ref, volt_ref, table_ref, norm_ref, pos_out, en_out):
    def sub_block(i, carry):
        rows = pl.ds(pl.multiple_of(i * SUB_ROWS, SUB_ROWS), SUB_ROWS)
        volts = volt_ref[rows, :]
        weighted = table_ref[0, rows, :] * volts[:, 0:1]
        for j in range(1, BINS):
            weighted = weighted + table_ref[j, rows, :] * volts[:, j : j + 1]
        energy = drift_ref[rows, :] - weighted / norm_ref[rows, :]
        en_out[rows, :] = energy
        pos_out[rows, :] = pos_ref[rows, :] + 0.25 * energy
        return carry

    lax.fori_loop(0, KICK_ROWS // SUB_ROWS, sub_block, 0)


def kick_call(positions, drifted, volt_rows, weights):
    table, norm = weights
    bunches, width = positions.shape
    wide = pl.BlockSpec((KICK_ROWS, width), lambda i: (i, 0))
    narrow = pl.BlockSpec((KICK_ROWS, BINS), lambda i: (i, 0))
    tall = pl.BlockSpec((BINS, KICK_ROWS, width), lambda i: (0, i, 0))
    shape = jax.ShapeDtypeStruct(positions.shape, jnp.float32)
    return pl.pallas_call(
        kick_kernel,
        grid=(bunches // KICK_ROWS,),
        in_specs=[wide, wide, narrow, tall, wide],
        out_specs=[wide, wide],
        out_shape=[shape, shape],
        cost_estimate=pl.CostEstimate(
            flops=2 * bunches * width * BINS,
            transcendentals=0,
            bytes_accessed=4 * bunches * (width * (BINS + 5) + BINS),
        ),
    )(positions, drifted, volt_rows, table, norm)


def on_device(positions, energies, bucket, impedance, history):
    groups = lax.axis_size("grp")
    domains = lax.axis_size("dom")
    group_index = lax.axis_index("grp")
    domain_index = lax.axis_index("dom")
    first_len = R1 * groups
    second_len = R2 * domains
    cycle_len = first_len * second_len * N3
    plane_len = second_len * N3
    depth_len = N3 // groups
    first_part = first_len // domains
    second_part = second_len // groups
    per_row = N3 // BINS
    row_buckets = second_len * per_row
    own_rows = R2 * per_row
    partial_value = jnp.sum(kernel_table(positions), axis=2) / float(P_DEV * domains)
    span = BUNCH_GRP // CHUNKS
    pieces = [slice(c * span, (c + 1) * span) for c in range(CHUNKS)]
    weights = []

    def covered(operand, axis_name, split_axis, concat_axis):
        piece = pieces[len(weights)]
        place, operand = lax.optimization_barrier((positions[piece], operand))
        got = exchange(operand, axis_name, split_axis, concat_axis)
        got, weight = lax.optimization_barrier((got, weight_call(place)))
        weights.append(weight)
        return got
    first_row = bucket // row_buckets
    within = bucket % row_buckets
    owner_dom = within // own_rows
    owned_here = owner_dom == domain_index
    slot = jnp.where(owned_here, first_row * own_rows + within - owner_dom * own_rows, -1)
    picker = (slot[None, :] == jnp.arange(R1 * own_rows, dtype=jnp.int32)[:, None]).astype(jnp.float32)
    totals = dom_sum(partial_value, domains)
    line_slab = contract("sb,bj->sj", picker, totals)
    density = line_slab.reshape(R1, R2, N3)
    first_table = block_table(first_len)
    second_table = block_table(second_len)
    third_table = block_table(N3)
    received = covered(density, "grp", 2, 0)
    rows = contract("nab,nok->oabk", received, first_table[0])
    second_global = domain_index * R2 + jnp.arange(R2, dtype=jnp.int32)
    depth_global = group_index * depth_len + jnp.arange(depth_len, dtype=jnp.int32)
    first_freq = jnp.arange(first_len, dtype=jnp.int32)
    cos_turn, sin_turn = rotation(
        first_freq[None, None, :]
        * (second_global[:, None, None] * N3 + depth_global[None, :, None]),
        cycle_len,
    )
    twist = turn(rows, cos_turn, -sin_turn)
    part = covered(twist, "dom", 3, 1)
    cols = contract("inbk,inom->obkm", part, second_table)
    second_freq = jnp.arange(second_len, dtype=jnp.int32)
    cos_turn, sin_turn = rotation(
        depth_global[:, None, None] * second_freq[None, None, :], plane_len
    )
    turned = turn(cols, cos_turn, -sin_turn)
    part = covered(turned, "grp", 3, 1)
    full = contract("inac,inok->oack", part, third_table)
    norm_factor = 1.0 / math.sqrt(BUNCH_GRP * groups)
    spectrum = full * norm_factor
    spec_real = spectrum[0]
    spec_imag = spectrum[1]
    volt_real = impedance[0, 0] * spec_real - impedance[0, 1] * spec_imag
    volt_imag = impedance[0, 0] * spec_imag + impedance[0, 1] * spec_real
    for earlier in range(HIST):
        past_real = history[earlier, 0]
        past_imag = history[earlier, 1]
        volt_real = (
            volt_real
            + impedance[earlier + 1, 0] * past_real
            - impedance[earlier + 1, 1] * past_imag
        )
        volt_imag = (
            volt_imag
            + impedance[earlier + 1, 0] * past_imag
            + impedance[earlier + 1, 1] * past_real
        )
    back = contract("iack,ikon->oacn", jnp.stack([volt_real, volt_imag]), conjugate(third_table))
    second_own = group_index * second_part + jnp.arange(second_part, dtype=jnp.int32)
    depth_all = jnp.arange(N3, dtype=jnp.int32)
    cos_turn, sin_turn = rotation(second_own[None, :, None] * depth_all[None, None, :], plane_len)
    lift = turn(back, cos_turn, sin_turn)
    part = covered(lift, "grp", 3, 2)
    spun = contract("iakb,ikon->oanb", part, conjugate(second_table))
    first_own = domain_index * first_part + jnp.arange(first_part, dtype=jnp.int32)
    cos_turn, sin_turn = rotation(
        first_own[:, None, None] * (second_freq[None, :, None] * N3 + depth_global[None, None, :]),
        cycle_len,
    )
    spin = turn(spun, cos_turn, sin_turn)
    inverse_factor = 1.0 / math.sqrt(cycle_len)
    part = exchange(spin, "dom", 2, 1)
    summed = contract("ikab,ikn->nab", part, conjugate(first_table)[:, :, 0, :])
    volt_part = summed * inverse_factor
    volt_slab = exchange(volt_part, "grp", 0, 2).reshape(
        R1 * own_rows, BINS
    )
    owned_volts = contract("sb,sj->bj", picker, volt_slab)
    volt_rows = dom_sum(owned_volts, domains)
    drifted = energies - 0.5 * jnp.sin(two_pi * (positions - 0.5 * BINS) / BINS)
    outs = [
        kick_call(positions[piece], drifted[piece], volt_rows[piece], weights[c])
        for c, piece in enumerate(pieces)
    ]
    positions_out = jnp.concatenate([o[0] for o in outs])
    energies_out = jnp.concatenate([o[1] for o in outs])
    return (positions_out, energies_out, spectrum)


def solution(mesh):
    placed = (
        P("grp", "dom"),
        P("grp", "dom"),
        P("grp"),
        P(None, None, "dom", "grp", None),
        P(None, None, "dom", "grp", None),
    )
    return jax.shard_map(
        on_device,
        mesh=mesh,
        in_specs=placed,
        out_specs=(P("grp", "dom"), P("grp", "dom"), P(None, "dom", "grp", None)),
        check_vma=False,
    )
```

```python
import math

import jax
import jax.numpy as jnp
from jax import lax
from jax.sharding import PartitionSpec as P
from jax.experimental import pallas as pl
from jax.experimental.pallas import tpu as pltpu

BINS = 32
N3 = 256
R1 = 8
R2 = 8
HIST = 2
BUNCH_GRP = 704
P_DEV = 256


highest = lax.Precision.HIGHEST
two_pi = 2.0 * math.pi
HALF_LOG2E = -0.5 / math.log(2.0)


def kernel_table(places):
    centers = jnp.arange(BINS, dtype=jnp.float32) + 0.5
    offset = places[:, None, :] - centers[None, :, None]
    return jnp.exp(-0.5 * offset * offset)


def dft_tables(length):
    series = jnp.arange(length, dtype=jnp.int32)
    windings = series[:, None] * series[None, :] % length
    angles = windings.astype(jnp.float32) * (two_pi / length)
    return (jnp.cos(angles), jnp.sin(angles))


def rotation(windings, modulus):
    angles = (windings % modulus).astype(jnp.float32) * (two_pi / modulus)
    return (jnp.cos(angles), jnp.sin(angles))


def contract(pattern, operand, matrix):
    return jnp.einsum(pattern, operand, matrix, precision=highest)


def block_table(length):
    cos_t, sin_t = dft_tables(length)
    return jnp.stack([jnp.stack([cos_t, -sin_t], axis=1), jnp.stack([sin_t, cos_t], axis=1)])


def conjugate(table):
    return table * jnp.array([1.0, -1.0], jnp.float32)[None, None, :, None] * jnp.array(
        [1.0, -1.0], jnp.float32
    )[:, None, None, None]


def turn(pair, cos_t, sin_t):
    return jnp.stack([pair[0] * cos_t - pair[1] * sin_t, pair[0] * sin_t + pair[1] * cos_t])


def exchange(x, axis_name, split_axis, concat_axis):
    count = lax.axis_size(axis_name)
    front = jnp.moveaxis(x, split_axis, 0)
    rest = front.shape[1:]
    piece = (front.shape[0] // count,) + rest
    sent = front.reshape(count, -1, 128)
    got = lax.all_to_all(sent, axis_name, 0, 0, tiled=True).reshape((count,) + piece)
    got = jnp.moveaxis(got, 1, split_axis + 1)
    got = jnp.moveaxis(got, 0, concat_axis)
    shape = list(x.shape)
    shape[split_axis] //= count
    shape[concat_axis] *= count
    return got.reshape(shape)


def dom_sum(rows, domains):
    chunk = rows.shape[0] // domains
    pieces = lax.all_to_all(rows.reshape(domains, -1, 128), "dom", 0, 0, tiled=True)
    mine = jnp.sum(pieces, axis=0)
    spread = jnp.broadcast_to(mine[None], (domains,) + mine.shape)
    return lax.all_to_all(spread, "dom", 0, 0, tiled=True).reshape(rows.shape)


KICK_ROWS = 64
SUB_ROWS = 8


def kick_kernel(pos_ref, drift_ref, volt_ref, pos_out, en_out):
    def sub_block(i, carry):
        rows = pl.ds(pl.multiple_of(i * SUB_ROWS, SUB_ROWS), SUB_ROWS)
        place = pos_ref[rows, :]
        volts = volt_ref[rows, :]
        weighted = jnp.zeros_like(place)
        norm = jnp.zeros_like(place)
        for j in range(BINS):
            offset = place - (j + 0.5)
            table = jnp.exp2(offset * offset * HALF_LOG2E)
            weighted = weighted + table * volts[:, j : j + 1]
            norm = norm + table
        energy = drift_ref[rows, :] - weighted / norm
        en_out[rows, :] = energy
        pos_out[rows, :] = place + 0.25 * energy
        return carry

    lax.fori_loop(0, KICK_ROWS // SUB_ROWS, sub_block, 0)


def kick_call(positions, drifted, volt_rows):
    bunches, width = positions.shape
    wide = pl.BlockSpec((KICK_ROWS, width), lambda i: (i, 0))
    narrow = pl.BlockSpec((KICK_ROWS, BINS), lambda i: (i, 0))
    shape = jax.ShapeDtypeStruct(positions.shape, jnp.float32)
    return pl.pallas_call(
        kick_kernel,
        grid=(bunches // KICK_ROWS,),
        in_specs=[wide, wide, narrow],
        out_specs=[wide, wide],
        out_shape=[shape, shape],
        cost_estimate=pl.CostEstimate(
            flops=12 * bunches * width * BINS,
            transcendentals=bunches * width * BINS,
            bytes_accessed=4 * bunches * (4 * width + BINS),
        ),
    )(positions, drifted, volt_rows)


def on_device(positions, energies, bucket, impedance, history):
    groups = lax.axis_size("grp")
    domains = lax.axis_size("dom")
    group_index = lax.axis_index("grp")
    domain_index = lax.axis_index("dom")
    first_len = R1 * groups
    second_len = R2 * domains
    cycle_len = first_len * second_len * N3
    plane_len = second_len * N3
    depth_len = N3 // groups
    first_part = first_len // domains
    second_part = second_len // groups
    per_row = N3 // BINS
    row_buckets = second_len * per_row
    own_rows = R2 * per_row
    partial_value = jnp.sum(kernel_table(positions), axis=2) / float(P_DEV * domains)
    first_row = bucket // row_buckets
    within = bucket % row_buckets
    owner_dom = within // own_rows
    owned_here = owner_dom == domain_index
    slot = jnp.where(owned_here, first_row * own_rows + within - owner_dom * own_rows, -1)
    picker = (slot[None, :] == jnp.arange(R1 * own_rows, dtype=jnp.int32)[:, None]).astype(jnp.float32)
    totals = dom_sum(partial_value, domains)
    line_slab = contract("sb,bj->sj", picker, totals)
    density = line_slab.reshape(R1, R2, N3)
    first_table = block_table(first_len)
    second_table = block_table(second_len)
    third_table = block_table(N3)
    received = exchange(density, "grp", 2, 0)
    rows = contract("nab,nok->oabk", received, first_table[0])
    second_global = domain_index * R2 + jnp.arange(R2, dtype=jnp.int32)
    depth_global = group_index * depth_len + jnp.arange(depth_len, dtype=jnp.int32)
    first_freq = jnp.arange(first_len, dtype=jnp.int32)
    cos_turn, sin_turn = rotation(
        first_freq[None, None, :]
        * (second_global[:, None, None] * N3 + depth_global[None, :, None]),
        cycle_len,
    )
    twist = turn(rows, cos_turn, -sin_turn)
    part = exchange(twist, "dom", 3, 1)
    cols = contract("inbk,inom->obkm", part, second_table)
    second_freq = jnp.arange(second_len, dtype=jnp.int32)
    cos_turn, sin_turn = rotation(
        depth_global[:, None, None] * second_freq[None, None, :], plane_len
    )
    turned = turn(cols, cos_turn, -sin_turn)
    part = exchange(turned, "grp", 3, 1)
    full = contract("inac,inok->oack", part, third_table)
    norm_factor = 1.0 / math.sqrt(BUNCH_GRP * groups)
    spectrum = full * norm_factor
    spec_real = spectrum[0]
    spec_imag = spectrum[1]
    volt_real = impedance[0, 0] * spec_real - impedance[0, 1] * spec_imag
    volt_imag = impedance[0, 0] * spec_imag + impedance[0, 1] * spec_real
    for earlier in range(HIST):
        past_real = history[earlier, 0]
        past_imag = history[earlier, 1]
        volt_real = (
            volt_real
            + impedance[earlier + 1, 0] * past_real
            - impedance[earlier + 1, 1] * past_imag
        )
        volt_imag = (
            volt_imag
            + impedance[earlier + 1, 0] * past_imag
            + impedance[earlier + 1, 1] * past_real
        )
    back = contract("iack,ikon->oacn", jnp.stack([volt_real, volt_imag]), conjugate(third_table))
    second_own = group_index * second_part + jnp.arange(second_part, dtype=jnp.int32)
    depth_all = jnp.arange(N3, dtype=jnp.int32)
    cos_turn, sin_turn = rotation(second_own[None, :, None] * depth_all[None, None, :], plane_len)
    lift = turn(back, cos_turn, sin_turn)
    part = exchange(lift, "grp", 3, 2)
    spun = contract("iakb,ikon->oanb", part, conjugate(second_table))
    first_own = domain_index * first_part + jnp.arange(first_part, dtype=jnp.int32)
    cos_turn, sin_turn = rotation(
        first_own[:, None, None] * (second_freq[None, :, None] * N3 + depth_global[None, None, :]),
        cycle_len,
    )
    spin = turn(spun, cos_turn, sin_turn)
    inverse_factor = 1.0 / math.sqrt(cycle_len)
    part = exchange(spin, "dom", 2, 1)
    summed = contract("ikab,ikn->nab", part, conjugate(first_table)[:, :, 0, :])
    volt_part = summed * inverse_factor
    volt_slab = exchange(volt_part, "grp", 0, 2).reshape(
        R1 * own_rows, BINS
    )
    owned_volts = contract("sb,sj->bj", picker, volt_slab)
    volt_rows = dom_sum(owned_volts, domains)
    drifted = energies - 0.5 * jnp.sin(two_pi * (positions - 0.5 * BINS) / BINS)
    positions_out, energies_out = kick_call(positions, drifted, volt_rows)
    return (positions_out, energies_out, spectrum)


def solution(mesh):
    placed = (
        P("grp", "dom"),
        P("grp", "dom"),
        P("grp"),
        P(None, None, "dom", "grp", None),
        P(None, None, "dom", "grp", None),
    )
    return jax.shard_map(
        on_device,
        mesh=mesh,
        in_specs=placed,
        out_specs=(P("grp", "dom"), P("grp", "dom"), P(None, "dom", "grp", None)),
        check_vma=False,
    )
```

```python
import math

import jax
import jax.numpy as jnp
from jax import lax
from jax.sharding import PartitionSpec as P
from jax.experimental import pallas as pl
from jax.experimental.pallas import tpu as pltpu

BINS = 32
N3 = 256
R1 = 8
R2 = 8
HIST = 2
BUNCH_GRP = 704
P_DEV = 256


highest = lax.Precision.HIGHEST
two_pi = 2.0 * math.pi
HALF_LOG2E = -0.5 / math.log(2.0)


def kernel_table(places):
    centers = jnp.arange(BINS, dtype=jnp.float32) + 0.5
    offset = places[:, None, :] - centers[None, :, None]
    return jnp.exp(-0.5 * offset * offset)


def dft_tables(length):
    series = jnp.arange(length, dtype=jnp.int32)
    windings = series[:, None] * series[None, :] % length
    angles = windings.astype(jnp.float32) * (two_pi / length)
    return (jnp.cos(angles), jnp.sin(angles))


def rotation(windings, modulus):
    angles = (windings % modulus).astype(jnp.float32) * (two_pi / modulus)
    return (jnp.cos(angles), jnp.sin(angles))


def contract(pattern, operand, matrix):
    return jnp.einsum(pattern, operand, matrix, precision=highest)


def block_table(length):
    cos_t, sin_t = dft_tables(length)
    return jnp.stack([jnp.stack([cos_t, -sin_t], axis=1), jnp.stack([sin_t, cos_t], axis=1)])


def conjugate(table):
    return table * jnp.array([1.0, -1.0], jnp.float32)[None, None, :, None] * jnp.array(
        [1.0, -1.0], jnp.float32
    )[:, None, None, None]


def turn(pair, cos_t, sin_t):
    return jnp.stack([pair[0] * cos_t - pair[1] * sin_t, pair[0] * sin_t + pair[1] * cos_t])


def exchange(x, axis_name, split_axis, concat_axis):
    count = lax.axis_size(axis_name)
    front = jnp.moveaxis(x, split_axis, 0)
    rest = front.shape[1:]
    piece = (front.shape[0] // count,) + rest
    sent = front.reshape(count, -1, 128)
    got = lax.all_to_all(sent, axis_name, 0, 0, tiled=True).reshape((count,) + piece)
    got = jnp.moveaxis(got, 1, split_axis + 1)
    got = jnp.moveaxis(got, 0, concat_axis)
    shape = list(x.shape)
    shape[split_axis] //= count
    shape[concat_axis] *= count
    return got.reshape(shape)


def dom_sum(rows, domains):
    chunk = rows.shape[0] // domains
    pieces = lax.all_to_all(rows.reshape(domains, -1, 128), "dom", 0, 0, tiled=True)
    mine = jnp.sum(pieces, axis=0)
    spread = jnp.broadcast_to(mine[None], (domains,) + mine.shape)
    return lax.all_to_all(spread, "dom", 0, 0, tiled=True).reshape(rows.shape)


KICK_ROWS = 352
SUB_ROWS = 32


def kick_kernel(pos_ref, drift_ref, volt_ref, pos_out, en_out):
    def sub_block(i, carry):
        rows = pl.ds(pl.multiple_of(i * SUB_ROWS, SUB_ROWS), SUB_ROWS)
        place = pos_ref[rows, :]
        volts = volt_ref[rows, :]
        weighted = jnp.zeros_like(place)
        norm = jnp.zeros_like(place)
        for j in range(BINS):
            offset = place - (j + 0.5)
            table = jnp.exp2(offset * offset * HALF_LOG2E)
            weighted = weighted + table * volts[:, j : j + 1]
            norm = norm + table
        energy = drift_ref[rows, :] - weighted / norm
        en_out[rows, :] = energy
        pos_out[rows, :] = place + 0.25 * energy
        return carry

    lax.fori_loop(0, KICK_ROWS // SUB_ROWS, sub_block, 0)


def kick_call(positions, drifted, volt_rows):
    bunches, width = positions.shape
    wide = pl.BlockSpec((KICK_ROWS, width), lambda i: (i, 0))
    narrow = pl.BlockSpec((KICK_ROWS, BINS), lambda i: (i, 0))
    shape = jax.ShapeDtypeStruct(positions.shape, jnp.float32)
    return pl.pallas_call(
        kick_kernel,
        grid=(bunches // KICK_ROWS,),
        in_specs=[wide, wide, narrow],
        out_specs=[wide, wide],
        out_shape=[shape, shape],
        cost_estimate=pl.CostEstimate(
            flops=12 * bunches * width * BINS,
            transcendentals=bunches * width * BINS,
            bytes_accessed=4 * bunches * (4 * width + BINS),
        ),
    )(positions, drifted, volt_rows)


def on_device(positions, energies, bucket, impedance, history):
    groups = lax.axis_size("grp")
    domains = lax.axis_size("dom")
    group_index = lax.axis_index("grp")
    domain_index = lax.axis_index("dom")
    first_len = R1 * groups
    second_len = R2 * domains
    cycle_len = first_len * second_len * N3
    plane_len = second_len * N3
    depth_len = N3 // groups
    first_part = first_len // domains
    second_part = second_len // groups
    per_row = N3 // BINS
    row_buckets = second_len * per_row
    own_rows = R2 * per_row
    partial_value = jnp.sum(kernel_table(positions), axis=2) / float(P_DEV * domains)
    first_row = bucket // row_buckets
    within = bucket % row_buckets
    owner_dom = within // own_rows
    owned_here = owner_dom == domain_index
    slot = jnp.where(owned_here, first_row * own_rows + within - owner_dom * own_rows, -1)
    picker = (slot[None, :] == jnp.arange(R1 * own_rows, dtype=jnp.int32)[:, None]).astype(jnp.float32)
    totals = dom_sum(partial_value, domains)
    line_slab = contract("sb,bj->sj", picker, totals)
    density = line_slab.reshape(R1, R2, N3)
    first_table = block_table(first_len)
    second_table = block_table(second_len)
    third_table = block_table(N3)
    received = exchange(density, "grp", 2, 0)
    rows = contract("nab,nok->oabk", received, first_table[0])
    second_global = domain_index * R2 + jnp.arange(R2, dtype=jnp.int32)
    depth_global = group_index * depth_len + jnp.arange(depth_len, dtype=jnp.int32)
    first_freq = jnp.arange(first_len, dtype=jnp.int32)
    cos_turn, sin_turn = rotation(
        first_freq[None, None, :]
        * (second_global[:, None, None] * N3 + depth_global[None, :, None]),
        cycle_len,
    )
    twist = turn(rows, cos_turn, -sin_turn)
    part = exchange(twist, "dom", 3, 1)
    cols = contract("inbk,inom->obkm", part, second_table)
    second_freq = jnp.arange(second_len, dtype=jnp.int32)
    cos_turn, sin_turn = rotation(
        depth_global[:, None, None] * second_freq[None, None, :], plane_len
    )
    turned = turn(cols, cos_turn, -sin_turn)
    part = exchange(turned, "grp", 3, 1)
    full = contract("inac,inok->oack", part, third_table)
    norm_factor = 1.0 / math.sqrt(BUNCH_GRP * groups)
    spectrum = full * norm_factor
    spec_real = spectrum[0]
    spec_imag = spectrum[1]
    volt_real = impedance[0, 0] * spec_real - impedance[0, 1] * spec_imag
    volt_imag = impedance[0, 0] * spec_imag + impedance[0, 1] * spec_real
    for earlier in range(HIST):
        past_real = history[earlier, 0]
        past_imag = history[earlier, 1]
        volt_real = (
            volt_real
            + impedance[earlier + 1, 0] * past_real
            - impedance[earlier + 1, 1] * past_imag
        )
        volt_imag = (
            volt_imag
            + impedance[earlier + 1, 0] * past_imag
            + impedance[earlier + 1, 1] * past_real
        )
    back = contract("iack,ikon->oacn", jnp.stack([volt_real, volt_imag]), conjugate(third_table))
    second_own = group_index * second_part + jnp.arange(second_part, dtype=jnp.int32)
    depth_all = jnp.arange(N3, dtype=jnp.int32)
    cos_turn, sin_turn = rotation(second_own[None, :, None] * depth_all[None, None, :], plane_len)
    lift = turn(back, cos_turn, sin_turn)
    part = exchange(lift, "grp", 3, 2)
    spun = contract("iakb,ikon->oanb", part, conjugate(second_table))
    first_own = domain_index * first_part + jnp.arange(first_part, dtype=jnp.int32)
    cos_turn, sin_turn = rotation(
        first_own[:, None, None] * (second_freq[None, :, None] * N3 + depth_global[None, None, :]),
        cycle_len,
    )
    spin = turn(spun, cos_turn, sin_turn)
    inverse_factor = 1.0 / math.sqrt(cycle_len)
    part = exchange(spin, "dom", 2, 1)
    summed = contract("ikab,ikn->nab", part, conjugate(first_table)[:, :, 0, :])
    volt_part = summed * inverse_factor
    volt_slab = exchange(volt_part, "grp", 0, 2).reshape(
        R1 * own_rows, BINS
    )
    owned_volts = contract("sb,sj->bj", picker, volt_slab)
    volt_rows = dom_sum(owned_volts, domains)
    drifted = energies - 0.5 * jnp.sin(two_pi * (positions - 0.5 * BINS) / BINS)
    positions_out, energies_out = kick_call(positions, drifted, volt_rows)
    return (positions_out, energies_out, spectrum)


def solution(mesh):
    placed = (
        P("grp", "dom"),
        P("grp", "dom"),
        P("grp"),
        P(None, None, "dom", "grp", None),
        P(None, None, "dom", "grp", None),
    )
    return jax.shard_map(
        on_device,
        mesh=mesh,
        in_specs=placed,
        out_specs=(P("grp", "dom"), P("grp", "dom"), P(None, "dom", "grp", None)),
        check_vma=False,
    )
```

```python
import math

import jax
import jax.numpy as jnp
from jax import lax
from jax.sharding import PartitionSpec as P
from jax.experimental import pallas as pl
from jax.experimental.pallas import tpu as pltpu

BINS = 32
N3 = 256
R1 = 8
R2 = 8
HIST = 2
BUNCH_GRP = 704
P_DEV = 256


highest = lax.Precision.HIGHEST
two_pi = 2.0 * math.pi
HALF_LOG2E = -0.5 / math.log(2.0)


def kernel_table(places):
    centers = jnp.arange(BINS, dtype=jnp.float32) + 0.5
    offset = places[:, None, :] - centers[None, :, None]
    return jnp.exp(-0.5 * offset * offset)


def dft_tables(length):
    series = jnp.arange(length, dtype=jnp.int32)
    windings = series[:, None] * series[None, :] % length
    angles = windings.astype(jnp.float32) * (two_pi / length)
    return (jnp.cos(angles), jnp.sin(angles))


def rotation(windings, modulus):
    angles = (windings % modulus).astype(jnp.float32) * (two_pi / modulus)
    return (jnp.cos(angles), jnp.sin(angles))


def contract(pattern, operand, matrix):
    return jnp.einsum(pattern, operand, matrix, precision=highest)


def block_table(length):
    cos_t, sin_t = dft_tables(length)
    return jnp.stack([jnp.stack([cos_t, -sin_t], axis=1), jnp.stack([sin_t, cos_t], axis=1)])


def conjugate(table):
    return table * jnp.array([1.0, -1.0], jnp.float32)[None, None, :, None] * jnp.array(
        [1.0, -1.0], jnp.float32
    )[:, None, None, None]


def turn(pair, cos_t, sin_t):
    return jnp.stack([pair[0] * cos_t - pair[1] * sin_t, pair[0] * sin_t + pair[1] * cos_t])


def exchange(x, axis_name, split_axis, concat_axis):
    count = lax.axis_size(axis_name)
    front = jnp.moveaxis(x, split_axis, 0)
    rest = front.shape[1:]
    piece = (front.shape[0] // count,) + rest
    sent = front.reshape(count, -1, 128)
    got = lax.all_to_all(sent, axis_name, 0, 0, tiled=True).reshape((count,) + piece)
    got = jnp.moveaxis(got, 1, split_axis + 1)
    got = jnp.moveaxis(got, 0, concat_axis)
    shape = list(x.shape)
    shape[split_axis] //= count
    shape[concat_axis] *= count
    return got.reshape(shape)


def dom_sum(rows, domains):
    chunk = rows.shape[0] // domains
    pieces = lax.all_to_all(rows.reshape(domains, -1, 128), "dom", 0, 0, tiled=True)
    mine = jnp.sum(pieces, axis=0)
    spread = jnp.broadcast_to(mine[None], (domains,) + mine.shape)
    return lax.all_to_all(spread, "dom", 0, 0, tiled=True).reshape(rows.shape)


KICK_ROWS = 352
SUB_ROWS = 32


def profile_kernel(pos_ref, out_ref):
    def sub_block(i, carry):
        rows = pl.ds(pl.multiple_of(i * SUB_ROWS, SUB_ROWS), SUB_ROWS)
        place = pos_ref[rows, :]
        for j in range(BINS):
            offset = place - (j + 0.5)
            table = jnp.exp(-0.5 * offset * offset)
            out_ref[rows, j : j + 1] = jnp.sum(table, axis=1, keepdims=True)
        return carry

    lax.fori_loop(0, KICK_ROWS // SUB_ROWS, sub_block, 0)


def profile_call(positions):
    bunches, width = positions.shape
    return pl.pallas_call(
        profile_kernel,
        grid=(bunches // KICK_ROWS,),
        in_specs=[pl.BlockSpec((KICK_ROWS, width), lambda i: (i, 0))],
        out_specs=pl.BlockSpec((KICK_ROWS, BINS), lambda i: (i, 0)),
        out_shape=jax.ShapeDtypeStruct((bunches, BINS), jnp.float32),
        cost_estimate=pl.CostEstimate(
            flops=5 * bunches * width * BINS,
            transcendentals=bunches * width * BINS,
            bytes_accessed=4 * bunches * (width + BINS),
        ),
    )(positions)


def kick_kernel(pos_ref, drift_ref, volt_ref, pos_out, en_out):
    def sub_block(i, carry):
        rows = pl.ds(pl.multiple_of(i * SUB_ROWS, SUB_ROWS), SUB_ROWS)
        place = pos_ref[rows, :]
        volts = volt_ref[rows, :]
        weighted = jnp.zeros_like(place)
        norm = jnp.zeros_like(place)
        for j in range(BINS):
            offset = place - (j + 0.5)
            table = jnp.exp2(offset * offset * HALF_LOG2E)
            weighted = weighted + table * volts[:, j : j + 1]
            norm = norm + table
        energy = drift_ref[rows, :] - weighted / norm
        en_out[rows, :] = energy
        pos_out[rows, :] = place + 0.25 * energy
        return carry

    lax.fori_loop(0, KICK_ROWS // SUB_ROWS, sub_block, 0)


def kick_call(positions, drifted, volt_rows):
    bunches, width = positions.shape
    wide = pl.BlockSpec((KICK_ROWS, width), lambda i: (i, 0))
    narrow = pl.BlockSpec((KICK_ROWS, BINS), lambda i: (i, 0))
    shape = jax.ShapeDtypeStruct(positions.shape, jnp.float32)
    return pl.pallas_call(
        kick_kernel,
        grid=(bunches // KICK_ROWS,),
        in_specs=[wide, wide, narrow],
        out_specs=[wide, wide],
        out_shape=[shape, shape],
        cost_estimate=pl.CostEstimate(
            flops=12 * bunches * width * BINS,
            transcendentals=bunches * width * BINS,
            bytes_accessed=4 * bunches * (4 * width + BINS),
        ),
    )(positions, drifted, volt_rows)


def on_device(positions, energies, bucket, impedance, history):
    groups = lax.axis_size("grp")
    domains = lax.axis_size("dom")
    group_index = lax.axis_index("grp")
    domain_index = lax.axis_index("dom")
    first_len = R1 * groups
    second_len = R2 * domains
    cycle_len = first_len * second_len * N3
    plane_len = second_len * N3
    depth_len = N3 // groups
    first_part = first_len // domains
    second_part = second_len // groups
    per_row = N3 // BINS
    row_buckets = second_len * per_row
    own_rows = R2 * per_row
    partial_value = profile_call(positions) / float(P_DEV * domains)
    first_row = bucket // row_buckets
    within = bucket % row_buckets
    owner_dom = within // own_rows
    owned_here = owner_dom == domain_index
    slot = jnp.where(owned_here, first_row * own_rows + within - owner_dom * own_rows, -1)
    picker = (slot[None, :] == jnp.arange(R1 * own_rows, dtype=jnp.int32)[:, None]).astype(jnp.float32)
    totals = dom_sum(partial_value, domains)
    line_slab = contract("sb,bj->sj", picker, totals)
    density = line_slab.reshape(R1, R2, N3)
    first_table = block_table(first_len)
    second_table = block_table(second_len)
    third_table = block_table(N3)
    received = exchange(density, "grp", 2, 0)
    rows = contract("nab,nok->oabk", received, first_table[0])
    second_global = domain_index * R2 + jnp.arange(R2, dtype=jnp.int32)
    depth_global = group_index * depth_len + jnp.arange(depth_len, dtype=jnp.int32)
    first_freq = jnp.arange(first_len, dtype=jnp.int32)
    cos_turn, sin_turn = rotation(
        first_freq[None, None, :]
        * (second_global[:, None, None] * N3 + depth_global[None, :, None]),
        cycle_len,
    )
    twist = turn(rows, cos_turn, -sin_turn)
    part = exchange(twist, "dom", 3, 1)
    cols = contract("inbk,inom->obkm", part, second_table)
    second_freq = jnp.arange(second_len, dtype=jnp.int32)
    cos_turn, sin_turn = rotation(
        depth_global[:, None, None] * second_freq[None, None, :], plane_len
    )
    turned = turn(cols, cos_turn, -sin_turn)
    part = exchange(turned, "grp", 3, 1)
    full = contract("inac,inok->oack", part, third_table)
    norm_factor = 1.0 / math.sqrt(BUNCH_GRP * groups)
    spectrum = full * norm_factor
    spec_real = spectrum[0]
    spec_imag = spectrum[1]
    volt_real = impedance[0, 0] * spec_real - impedance[0, 1] * spec_imag
    volt_imag = impedance[0, 0] * spec_imag + impedance[0, 1] * spec_real
    for earlier in range(HIST):
        past_real = history[earlier, 0]
        past_imag = history[earlier, 1]
        volt_real = (
            volt_real
            + impedance[earlier + 1, 0] * past_real
            - impedance[earlier + 1, 1] * past_imag
        )
        volt_imag = (
            volt_imag
            + impedance[earlier + 1, 0] * past_imag
            + impedance[earlier + 1, 1] * past_real
        )
    back = contract("iack,ikon->oacn", jnp.stack([volt_real, volt_imag]), conjugate(third_table))
    second_own = group_index * second_part + jnp.arange(second_part, dtype=jnp.int32)
    depth_all = jnp.arange(N3, dtype=jnp.int32)
    cos_turn, sin_turn = rotation(second_own[None, :, None] * depth_all[None, None, :], plane_len)
    lift = turn(back, cos_turn, sin_turn)
    part = exchange(lift, "grp", 3, 2)
    spun = contract("iakb,ikon->oanb", part, conjugate(second_table))
    first_own = domain_index * first_part + jnp.arange(first_part, dtype=jnp.int32)
    cos_turn, sin_turn = rotation(
        first_own[:, None, None] * (second_freq[None, :, None] * N3 + depth_global[None, None, :]),
        cycle_len,
    )
    spin = turn(spun, cos_turn, sin_turn)
    inverse_factor = 1.0 / math.sqrt(cycle_len)
    part = exchange(spin, "dom", 2, 1)
    summed = contract("ikab,ikn->nab", part, conjugate(first_table)[:, :, 0, :])
    volt_part = summed * inverse_factor
    volt_slab = exchange(volt_part, "grp", 0, 2).reshape(
        R1 * own_rows, BINS
    )
    owned_volts = contract("sb,sj->bj", picker, volt_slab)
    volt_rows = dom_sum(owned_volts, domains)
    drifted = energies - 0.5 * jnp.sin(two_pi * (positions - 0.5 * BINS) / BINS)
    positions_out, energies_out = kick_call(positions, drifted, volt_rows)
    return (positions_out, energies_out, spectrum)


def solution(mesh):
    placed = (
        P("grp", "dom"),
        P("grp", "dom"),
        P("grp"),
        P(None, None, "dom", "grp", None),
        P(None, None, "dom", "grp", None),
    )
    return jax.shard_map(
        on_device,
        mesh=mesh,
        in_specs=placed,
        out_specs=(P("grp", "dom"), P("grp", "dom"), P(None, "dom", "grp", None)),
        check_vma=False,
    )
```

```python
import math

import jax
import jax.numpy as jnp
from jax import lax
from jax.sharding import PartitionSpec as P
from jax.experimental import pallas as pl
from jax.experimental.pallas import tpu as pltpu

BINS = 32
N3 = 256
R1 = 8
R2 = 8
HIST = 2
BUNCH_GRP = 704
P_DEV = 256


highest = lax.Precision.HIGHEST
two_pi = 2.0 * math.pi
HALF_LOG2E = -0.5 / math.log(2.0)


def kernel_table(places):
    centers = jnp.arange(BINS, dtype=jnp.float32) + 0.5
    offset = places[:, None, :] - centers[None, :, None]
    return jnp.exp(-0.5 * offset * offset)


def dft_tables(length):
    series = jnp.arange(length, dtype=jnp.int32)
    windings = series[:, None] * series[None, :] % length
    angles = windings.astype(jnp.float32) * (two_pi / length)
    return (jnp.cos(angles), jnp.sin(angles))


def rotation(windings, modulus):
    angles = (windings % modulus).astype(jnp.float32) * (two_pi / modulus)
    return (jnp.cos(angles), jnp.sin(angles))


def contract(pattern, operand, matrix):
    return jnp.einsum(pattern, operand, matrix, precision=highest)


def block_table(length):
    cos_t, sin_t = dft_tables(length)
    return jnp.stack([jnp.stack([cos_t, -sin_t], axis=1), jnp.stack([sin_t, cos_t], axis=1)])


def conjugate(table):
    return table * jnp.array([1.0, -1.0], jnp.float32)[None, None, :, None] * jnp.array(
        [1.0, -1.0], jnp.float32
    )[:, None, None, None]


def turn(pair, cos_t, sin_t):
    return jnp.stack([pair[0] * cos_t - pair[1] * sin_t, pair[0] * sin_t + pair[1] * cos_t])


def exchange(x, axis_name, split_axis, concat_axis):
    count = lax.axis_size(axis_name)
    front = jnp.moveaxis(x, split_axis, 0)
    rest = front.shape[1:]
    piece = (front.shape[0] // count,) + rest
    sent = front.reshape(count, -1, 128)
    got = lax.all_to_all(sent, axis_name, 0, 0, tiled=True).reshape((count,) + piece)
    got = jnp.moveaxis(got, 1, split_axis + 1)
    got = jnp.moveaxis(got, 0, concat_axis)
    shape = list(x.shape)
    shape[split_axis] //= count
    shape[concat_axis] *= count
    return got.reshape(shape)


def dom_sum(rows, domains):
    chunk = rows.shape[0] // domains
    pieces = lax.all_to_all(rows.reshape(domains, -1, 128), "dom", 0, 0, tiled=True)
    mine = jnp.sum(pieces, axis=0)
    spread = jnp.broadcast_to(mine[None], (domains,) + mine.shape)
    return lax.all_to_all(spread, "dom", 0, 0, tiled=True).reshape(rows.shape)


KICK_ROWS = 352
SUB_ROWS = 32


def kick_kernel(pos_ref, drift_ref, volt_ref, pos_out, en_out):
    def sub_block(i, carry):
        rows = pl.ds(pl.multiple_of(i * SUB_ROWS, SUB_ROWS), SUB_ROWS)
        place = pos_ref[rows, :]
        volts = volt_ref[rows, :]
        weighted = jnp.zeros_like(place)
        norm = jnp.zeros_like(place)
        for j in range(BINS):
            offset = place - (j + 0.5)
            table = jnp.exp2(offset * offset * HALF_LOG2E)
            weighted = weighted + table * volts[:, j : j + 1]
            norm = norm + table
        energy = drift_ref[rows, :] - weighted / norm
        en_out[rows, :] = energy
        pos_out[rows, :] = place + 0.25 * energy
        return carry

    lax.fori_loop(0, KICK_ROWS // SUB_ROWS, sub_block, 0, unroll=True)


def kick_call(positions, drifted, volt_rows):
    bunches, width = positions.shape
    wide = pl.BlockSpec((KICK_ROWS, width), lambda i: (i, 0))
    narrow = pl.BlockSpec((KICK_ROWS, BINS), lambda i: (i, 0))
    shape = jax.ShapeDtypeStruct(positions.shape, jnp.float32)
    return pl.pallas_call(
        kick_kernel,
        grid=(bunches // KICK_ROWS,),
        in_specs=[wide, wide, narrow],
        out_specs=[wide, wide],
        out_shape=[shape, shape],
        cost_estimate=pl.CostEstimate(
            flops=12 * bunches * width * BINS,
            transcendentals=bunches * width * BINS,
            bytes_accessed=4 * bunches * (4 * width + BINS),
        ),
    )(positions, drifted, volt_rows)


def on_device(positions, energies, bucket, impedance, history):
    groups = lax.axis_size("grp")
    domains = lax.axis_size("dom")
    group_index = lax.axis_index("grp")
    domain_index = lax.axis_index("dom")
    first_len = R1 * groups
    second_len = R2 * domains
    cycle_len = first_len * second_len * N3
    plane_len = second_len * N3
    depth_len = N3 // groups
    first_part = first_len // domains
    second_part = second_len // groups
    per_row = N3 // BINS
    row_buckets = second_len * per_row
    own_rows = R2 * per_row
    partial_value = jnp.sum(kernel_table(positions), axis=2) / float(P_DEV * domains)
    first_row = bucket // row_buckets
    within = bucket % row_buckets
    owner_dom = within // own_rows
    owned_here = owner_dom == domain_index
    slot = jnp.where(owned_here, first_row * own_rows + within - owner_dom * own_rows, -1)
    picker = (slot[None, :] == jnp.arange(R1 * own_rows, dtype=jnp.int32)[:, None]).astype(jnp.float32)
    totals = dom_sum(partial_value, domains)
    line_slab = contract("sb,bj->sj", picker, totals)
    density = line_slab.reshape(R1, R2, N3)
    first_table = block_table(first_len)
    second_table = block_table(second_len)
    third_table = block_table(N3)
    received = exchange(density, "grp", 2, 0)
    rows = contract("nab,nok->oabk", received, first_table[0])
    second_global = domain_index * R2 + jnp.arange(R2, dtype=jnp.int32)
    depth_global = group_index * depth_len + jnp.arange(depth_len, dtype=jnp.int32)
    first_freq = jnp.arange(first_len, dtype=jnp.int32)
    cos_turn, sin_turn = rotation(
        first_freq[None, None, :]
        * (second_global[:, None, None] * N3 + depth_global[None, :, None]),
        cycle_len,
    )
    twist = turn(rows, cos_turn, -sin_turn)
    part = exchange(twist, "dom", 3, 1)
    cols = contract("inbk,inom->obkm", part, second_table)
    second_freq = jnp.arange(second_len, dtype=jnp.int32)
    cos_turn, sin_turn = rotation(
        depth_global[:, None, None] * second_freq[None, None, :], plane_len
    )
    turned = turn(cols, cos_turn, -sin_turn)
    part = exchange(turned, "grp", 3, 1)
    full = contract("inac,inok->oack", part, third_table)
    norm_factor = 1.0 / math.sqrt(BUNCH_GRP * groups)
    spectrum = full * norm_factor
    spec_real = spectrum[0]
    spec_imag = spectrum[1]
    volt_real = impedance[0, 0] * spec_real - impedance[0, 1] * spec_imag
    volt_imag = impedance[0, 0] * spec_imag + impedance[0, 1] * spec_real
    for earlier in range(HIST):
        past_real = history[earlier, 0]
        past_imag = history[earlier, 1]
        volt_real = (
            volt_real
            + impedance[earlier + 1, 0] * past_real
            - impedance[earlier + 1, 1] * past_imag
        )
        volt_imag = (
            volt_imag
            + impedance[earlier + 1, 0] * past_imag
            + impedance[earlier + 1, 1] * past_real
        )
    back = contract("iack,ikon->oacn", jnp.stack([volt_real, volt_imag]), conjugate(third_table))
    second_own = group_index * second_part + jnp.arange(second_part, dtype=jnp.int32)
    depth_all = jnp.arange(N3, dtype=jnp.int32)
    cos_turn, sin_turn = rotation(second_own[None, :, None] * depth_all[None, None, :], plane_len)
    lift = turn(back, cos_turn, sin_turn)
    part = exchange(lift, "grp", 3, 2)
    spun = contract("iakb,ikon->oanb", part, conjugate(second_table))
    first_own = domain_index * first_part + jnp.arange(first_part, dtype=jnp.int32)
    cos_turn, sin_turn = rotation(
        first_own[:, None, None] * (second_freq[None, :, None] * N3 + depth_global[None, None, :]),
        cycle_len,
    )
    spin = turn(spun, cos_turn, sin_turn)
    inverse_factor = 1.0 / math.sqrt(cycle_len)
    part = exchange(spin, "dom", 2, 1)
    summed = contract("ikab,ikn->nab", part, conjugate(first_table)[:, :, 0, :])
    volt_part = summed * inverse_factor
    volt_slab = exchange(volt_part, "grp", 0, 2).reshape(
        R1 * own_rows, BINS
    )
    owned_volts = contract("sb,sj->bj", picker, volt_slab)
    volt_rows = dom_sum(owned_volts, domains)
    drifted = energies - 0.5 * jnp.sin(two_pi * (positions - 0.5 * BINS) / BINS)
    positions_out, energies_out = kick_call(positions, drifted, volt_rows)
    return (positions_out, energies_out, spectrum)


def solution(mesh):
    placed = (
        P("grp", "dom"),
        P("grp", "dom"),
        P("grp"),
        P(None, None, "dom", "grp", None),
        P(None, None, "dom", "grp", None),
    )
    return jax.shard_map(
        on_device,
        mesh=mesh,
        in_specs=placed,
        out_specs=(P("grp", "dom"), P("grp", "dom"), P(None, "dom", "grp", None)),
        check_vma=False,
    )
```

```python
import math

import jax
import jax.numpy as jnp
from jax import lax
from jax.sharding import PartitionSpec as P
from jax.experimental import pallas as pl
from jax.experimental.pallas import tpu as pltpu

BINS = 32
N3 = 256
R1 = 8
R2 = 8
HIST = 2
BUNCH_GRP = 704
P_DEV = 256


highest = lax.Precision.HIGHEST
two_pi = 2.0 * math.pi
HALF_LOG2E = -0.5 / math.log(2.0)


def kernel_table(places):
    centers = jnp.arange(BINS, dtype=jnp.float32) + 0.5
    offset = places[:, None, :] - centers[None, :, None]
    return jnp.exp(-0.5 * offset * offset)


def dft_tables(length):
    series = jnp.arange(length, dtype=jnp.int32)
    windings = series[:, None] * series[None, :] % length
    angles = windings.astype(jnp.float32) * (two_pi / length)
    return (jnp.cos(angles), jnp.sin(angles))


def rotation(windings, modulus):
    angles = (windings % modulus).astype(jnp.float32) * (two_pi / modulus)
    return (jnp.cos(angles), jnp.sin(angles))


def contract(pattern, operand, matrix):
    return jnp.einsum(pattern, operand, matrix, precision=highest)


def block_table(length):
    cos_t, sin_t = dft_tables(length)
    return jnp.stack([jnp.stack([cos_t, -sin_t], axis=1), jnp.stack([sin_t, cos_t], axis=1)])


def conjugate(table):
    return table * jnp.array([1.0, -1.0], jnp.float32)[None, None, :, None] * jnp.array(
        [1.0, -1.0], jnp.float32
    )[:, None, None, None]


def turn(pair, cos_t, sin_t):
    return jnp.stack([pair[0] * cos_t - pair[1] * sin_t, pair[0] * sin_t + pair[1] * cos_t])


def exchange(x, axis_name, split_axis, concat_axis):
    count = lax.axis_size(axis_name)
    front = jnp.moveaxis(x, split_axis, 0)
    rest = front.shape[1:]
    piece = (front.shape[0] // count,) + rest
    sent = front.reshape(count, -1, 128)
    got = lax.all_to_all(sent, axis_name, 0, 0, tiled=True).reshape((count,) + piece)
    got = jnp.moveaxis(got, 1, split_axis + 1)
    got = jnp.moveaxis(got, 0, concat_axis)
    shape = list(x.shape)
    shape[split_axis] //= count
    shape[concat_axis] *= count
    return got.reshape(shape)


def dom_sum(rows, domains):
    chunk = rows.shape[0] // domains
    pieces = lax.all_to_all(rows.reshape(domains, -1, 128), "dom", 0, 0, tiled=True)
    mine = jnp.sum(pieces, axis=0)
    spread = jnp.broadcast_to(mine[None], (domains,) + mine.shape)
    return lax.all_to_all(spread, "dom", 0, 0, tiled=True).reshape(rows.shape)


KICK_ROWS = 352
SUB_ROWS = 32


def kick_kernel(pos_ref, drift_ref, volt_ref, pos_out, en_out):
    def sub_block(i, carry):
        rows = pl.ds(pl.multiple_of(i * SUB_ROWS, SUB_ROWS), SUB_ROWS)
        place = pos_ref[rows, :]
        volts = volt_ref[rows, :]
        weighted = jnp.zeros_like(place)
        norm = jnp.zeros_like(place)
        for j in range(BINS):
            offset = place - (j + 0.5)
            table = jnp.exp2(offset * offset * HALF_LOG2E)
            weighted = weighted + table * volts[:, j : j + 1]
            norm = norm + table
        energy = drift_ref[rows, :] - weighted / norm
        en_out[rows, :] = energy
        pos_out[rows, :] = place + 0.25 * energy
        return carry

    lax.fori_loop(0, KICK_ROWS // SUB_ROWS, sub_block, 0)


def kick_call(positions, drifted, volt_rows):
    bunches, width = positions.shape
    wide = pl.BlockSpec((KICK_ROWS, width), lambda i: (i, 0))
    narrow = pl.BlockSpec((KICK_ROWS, BINS), lambda i: (i, 0))
    shape = jax.ShapeDtypeStruct(positions.shape, jnp.float32)
    return pl.pallas_call(
        kick_kernel,
        grid=(bunches // KICK_ROWS,),
        in_specs=[wide, wide, narrow],
        out_specs=[wide, wide],
        out_shape=[shape, shape],
        cost_estimate=pl.CostEstimate(
            flops=12 * bunches * width * BINS,
            transcendentals=bunches * width * BINS,
            bytes_accessed=4 * bunches * (4 * width + BINS),
        ),
    )(positions, drifted, volt_rows)


def on_device(positions, energies, bucket, impedance, history):
    groups = lax.axis_size("grp")
    domains = lax.axis_size("dom")
    group_index = lax.axis_index("grp")
    domain_index = lax.axis_index("dom")
    first_len = R1 * groups
    second_len = R2 * domains
    cycle_len = first_len * second_len * N3
    plane_len = second_len * N3
    depth_len = N3 // groups
    first_part = first_len // domains
    second_part = second_len // groups
    per_row = N3 // BINS
    row_buckets = second_len * per_row
    own_rows = R2 * per_row
    partial_value = jnp.sum(kernel_table(positions), axis=2) / float(P_DEV * domains)
    first_row = bucket // row_buckets
    within = bucket % row_buckets
    owner_dom = within // own_rows
    owned_here = owner_dom == domain_index
    slot = jnp.where(owned_here, first_row * own_rows + within - owner_dom * own_rows, -1)
    picker = (slot[None, :] == jnp.arange(R1 * own_rows, dtype=jnp.int32)[:, None]).astype(jnp.float32)
    totals = dom_sum(partial_value, domains)
    in_row = within % per_row
    row_key = jnp.where(owned_here, in_row * R1 + first_row, -1)
    row_picker = (row_key[None, :] == jnp.arange(per_row * R1, dtype=jnp.int32)[:, None]).astype(jnp.float32)
    lane_slot = (within - owner_dom * own_rows) // per_row
    half = BINS // 2
    lane_match = lane_slot[:, None] == (jnp.arange(128, dtype=jnp.int32) // half)[None, :]
    halves = [
        contract(
            "sb,bl->sl",
            row_picker,
            jnp.where(lane_match, jnp.tile(totals[:, h * half : (h + 1) * half], (1, 128 // half)), 0.0),
        ).reshape(per_row, R1, 128)
        for h in range(2)
    ]
    send = jnp.stack(halves, axis=1).reshape(groups, R1, 128)
    first_table = block_table(first_len)
    second_table = block_table(second_len)
    third_table = block_table(N3)
    received = lax.all_to_all(send, "grp", 0, 0, tiled=True).reshape(first_len, R2, depth_len)
    rows = contract("nab,nok->oabk", received, first_table[0])
    second_global = domain_index * R2 + jnp.arange(R2, dtype=jnp.int32)
    depth_global = group_index * depth_len + jnp.arange(depth_len, dtype=jnp.int32)
    first_freq = jnp.arange(first_len, dtype=jnp.int32)
    cos_turn, sin_turn = rotation(
        first_freq[None, None, :]
        * (second_global[:, None, None] * N3 + depth_global[None, :, None]),
        cycle_len,
    )
    twist = turn(rows, cos_turn, -sin_turn)
    part = exchange(twist, "dom", 3, 1)
    cols = contract("inbk,inom->obkm", part, second_table)
    second_freq = jnp.arange(second_len, dtype=jnp.int32)
    cos_turn, sin_turn = rotation(
        depth_global[:, None, None] * second_freq[None, None, :], plane_len
    )
    turned = turn(cols, cos_turn, -sin_turn)
    part = exchange(turned, "grp", 3, 1)
    full = contract("inac,inok->oack", part, third_table)
    norm_factor = 1.0 / math.sqrt(BUNCH_GRP * groups)
    spectrum = full * norm_factor
    spec_real = spectrum[0]
    spec_imag = spectrum[1]
    volt_real = impedance[0, 0] * spec_real - impedance[0, 1] * spec_imag
    volt_imag = impedance[0, 0] * spec_imag + impedance[0, 1] * spec_real
    for earlier in range(HIST):
        past_real = history[earlier, 0]
        past_imag = history[earlier, 1]
        volt_real = (
            volt_real
            + impedance[earlier + 1, 0] * past_real
            - impedance[earlier + 1, 1] * past_imag
        )
        volt_imag = (
            volt_imag
            + impedance[earlier + 1, 0] * past_imag
            + impedance[earlier + 1, 1] * past_real
        )
    back = contract("iack,ikon->oacn", jnp.stack([volt_real, volt_imag]), conjugate(third_table))
    second_own = group_index * second_part + jnp.arange(second_part, dtype=jnp.int32)
    depth_all = jnp.arange(N3, dtype=jnp.int32)
    cos_turn, sin_turn = rotation(second_own[None, :, None] * depth_all[None, None, :], plane_len)
    lift = turn(back, cos_turn, sin_turn)
    part = exchange(lift, "grp", 3, 2)
    spun = contract("iakb,ikon->oanb", part, conjugate(second_table))
    first_own = domain_index * first_part + jnp.arange(first_part, dtype=jnp.int32)
    cos_turn, sin_turn = rotation(
        first_own[:, None, None] * (second_freq[None, :, None] * N3 + depth_global[None, None, :]),
        cycle_len,
    )
    spin = turn(spun, cos_turn, sin_turn)
    inverse_factor = 1.0 / math.sqrt(cycle_len)
    part = exchange(spin, "dom", 2, 1)
    summed = contract("ikab,ikn->nab", part, conjugate(first_table)[:, :, 0, :])
    volt_part = summed * inverse_factor
    volt_slab = exchange(volt_part, "grp", 0, 2).reshape(
        R1 * own_rows, BINS
    )
    owned_volts = contract("sb,sj->bj", picker, volt_slab)
    volt_rows = dom_sum(owned_volts, domains)
    drifted = energies - 0.5 * jnp.sin(two_pi * (positions - 0.5 * BINS) / BINS)
    positions_out, energies_out = kick_call(positions, drifted, volt_rows)
    return (positions_out, energies_out, spectrum)


def solution(mesh):
    placed = (
        P("grp", "dom"),
        P("grp", "dom"),
        P("grp"),
        P(None, None, "dom", "grp", None),
        P(None, None, "dom", "grp", None),
    )
    return jax.shard_map(
        on_device,
        mesh=mesh,
        in_specs=placed,
        out_specs=(P("grp", "dom"), P("grp", "dom"), P(None, "dom", "grp", None)),
        check_vma=False,
    )
```

```python
import math

import jax
import jax.numpy as jnp
from jax import lax
from jax.sharding import PartitionSpec as P
from jax.experimental import pallas as pl
from jax.experimental.pallas import tpu as pltpu

BINS = 32
N3 = 256
R1 = 8
R2 = 8
HIST = 2
BUNCH_GRP = 704
P_DEV = 256


highest = lax.Precision.HIGHEST
two_pi = 2.0 * math.pi
HALF_LOG2E = -0.5 / math.log(2.0)


def kernel_table(places):
    centers = jnp.arange(BINS, dtype=jnp.float32) + 0.5
    offset = places[:, None, :] - centers[None, :, None]
    return jnp.exp(-0.5 * offset * offset)


def dft_tables(length):
    series = jnp.arange(length, dtype=jnp.int32)
    windings = series[:, None] * series[None, :] % length
    angles = windings.astype(jnp.float32) * (two_pi / length)
    return (jnp.cos(angles), jnp.sin(angles))


def rotation(windings, modulus):
    angles = (windings % modulus).astype(jnp.float32) * (two_pi / modulus)
    return (jnp.cos(angles), jnp.sin(angles))


def contract(pattern, operand, matrix):
    return jnp.einsum(pattern, operand, matrix, precision=highest)


def block_table(length):
    cos_t, sin_t = dft_tables(length)
    return jnp.stack([jnp.stack([cos_t, -sin_t], axis=1), jnp.stack([sin_t, cos_t], axis=1)])


def conjugate(table):
    return table * jnp.array([1.0, -1.0], jnp.float32)[None, None, :, None] * jnp.array(
        [1.0, -1.0], jnp.float32
    )[:, None, None, None]


def turn(pair, cos_t, sin_t):
    return jnp.stack([pair[0] * cos_t - pair[1] * sin_t, pair[0] * sin_t + pair[1] * cos_t])


def exchange(x, axis_name, split_axis, concat_axis):
    count = lax.axis_size(axis_name)
    front = jnp.moveaxis(x, split_axis, 0)
    rest = front.shape[1:]
    piece = (front.shape[0] // count,) + rest
    sent = front.reshape(count, -1, 128)
    got = lax.all_to_all(sent, axis_name, 0, 0, tiled=True).reshape((count,) + piece)
    got = jnp.moveaxis(got, 1, split_axis + 1)
    got = jnp.moveaxis(got, 0, concat_axis)
    shape = list(x.shape)
    shape[split_axis] //= count
    shape[concat_axis] *= count
    return got.reshape(shape)


def dom_sum(rows, domains):
    chunk = rows.shape[0] // domains
    pieces = lax.all_to_all(rows.reshape(domains, -1, 128), "dom", 0, 0, tiled=True)
    mine = jnp.sum(pieces, axis=0)
    spread = jnp.broadcast_to(mine[None], (domains,) + mine.shape)
    return lax.all_to_all(spread, "dom", 0, 0, tiled=True).reshape(rows.shape)


KICK_ROWS = 352
SUB_ROWS = 32


def kick_kernel(pos_ref, drift_ref, volt_ref, pos_out, en_out):
    def sub_block(i, carry):
        rows = pl.ds(pl.multiple_of(i * SUB_ROWS, SUB_ROWS), SUB_ROWS)
        place = pos_ref[rows, :]
        volts = volt_ref[rows, :]
        weighted = jnp.zeros_like(place)
        norm = jnp.zeros_like(place)
        for j in range(BINS):
            offset = place - (j + 0.5)
            table = jnp.exp2(offset * offset * HALF_LOG2E)
            weighted = weighted + table * volts[:, j : j + 1]
            norm = norm + table
        energy = drift_ref[rows, :] - weighted / norm
        en_out[rows, :] = energy
        pos_out[rows, :] = place + 0.25 * energy
        return carry

    lax.fori_loop(0, KICK_ROWS // SUB_ROWS, sub_block, 0)


def kick_call(positions, drifted, volt_rows):
    bunches, width = positions.shape
    wide = pl.BlockSpec((KICK_ROWS, width), lambda i: (i, 0))
    narrow = pl.BlockSpec((KICK_ROWS, BINS), lambda i: (i, 0))
    shape = jax.ShapeDtypeStruct(positions.shape, jnp.float32)
    return pl.pallas_call(
        kick_kernel,
        grid=(bunches // KICK_ROWS,),
        in_specs=[wide, wide, narrow],
        out_specs=[wide, wide],
        out_shape=[shape, shape],
        cost_estimate=pl.CostEstimate(
            flops=12 * bunches * width * BINS,
            transcendentals=bunches * width * BINS,
            bytes_accessed=4 * bunches * (4 * width + BINS),
        ),
    )(positions, drifted, volt_rows)


def on_device(positions, energies, bucket, impedance, history):
    groups = lax.axis_size("grp")
    domains = lax.axis_size("dom")
    group_index = lax.axis_index("grp")
    domain_index = lax.axis_index("dom")
    first_len = R1 * groups
    second_len = R2 * domains
    cycle_len = first_len * second_len * N3
    plane_len = second_len * N3
    depth_len = N3 // groups
    first_part = first_len // domains
    second_part = second_len // groups
    per_row = N3 // BINS
    row_buckets = second_len * per_row
    own_rows = R2 * per_row
    partial_value = jnp.sum(kernel_table(positions), axis=2) / float(P_DEV * domains)
    first_row = bucket // row_buckets
    within = bucket % row_buckets
    owner_dom = within // own_rows
    owned_here = owner_dom == domain_index
    slot = jnp.where(owned_here, first_row * own_rows + within - owner_dom * own_rows, -1)
    picker = (slot[None, :] == jnp.arange(R1 * own_rows, dtype=jnp.int32)[:, None]).astype(jnp.float32)
    totals = dom_sum(partial_value, domains)
    in_row = within % per_row
    row_key = jnp.where(owned_here, in_row * R1 + first_row, -1)
    row_picker = (row_key[None, :] == jnp.arange(per_row * R1, dtype=jnp.int32)[:, None]).astype(jnp.float32)
    lane_slot = (within - owner_dom * own_rows) // per_row
    half = BINS // 2
    lane_match = lane_slot[:, None] == (jnp.arange(128, dtype=jnp.int32) // half)[None, :]
    halves = [
        contract(
            "sb,bl->sl",
            row_picker,
            jnp.where(lane_match, jnp.tile(totals[:, h * half : (h + 1) * half], (1, 128 // half)), 0.0),
        ).reshape(per_row, R1, 128)
        for h in range(2)
    ]
    send = jnp.stack(halves, axis=1).reshape(groups, R1, 128)
    first_table = block_table(first_len)
    second_table = block_table(second_len)
    third_table = block_table(N3)
    received = lax.all_to_all(send, "grp", 0, 0, tiled=True).reshape(first_len, R2, depth_len)
    rows = contract("nab,nok->oabk", received, first_table[0])
    second_global = domain_index * R2 + jnp.arange(R2, dtype=jnp.int32)
    depth_global = group_index * depth_len + jnp.arange(depth_len, dtype=jnp.int32)
    first_freq = jnp.arange(first_len, dtype=jnp.int32)
    cos_turn, sin_turn = rotation(
        first_freq[None, None, :]
        * (second_global[:, None, None] * N3 + depth_global[None, :, None]),
        cycle_len,
    )
    twist = turn(rows, cos_turn, -sin_turn)
    part = exchange(twist, "dom", 3, 1)
    cols = contract("inbk,inom->obkm", part, second_table)
    second_freq = jnp.arange(second_len, dtype=jnp.int32)
    cos_turn, sin_turn = rotation(
        depth_global[:, None, None] * second_freq[None, None, :], plane_len
    )
    turned = turn(cols, cos_turn, -sin_turn)
    part = exchange(turned, "grp", 3, 1)
    full = contract("inac,inok->oack", part, third_table)
    norm_factor = 1.0 / math.sqrt(BUNCH_GRP * groups)
    spectrum = full * norm_factor
    spec_real = spectrum[0]
    spec_imag = spectrum[1]
    volt_real = impedance[0, 0] * spec_real - impedance[0, 1] * spec_imag
    volt_imag = impedance[0, 0] * spec_imag + impedance[0, 1] * spec_real
    for earlier in range(HIST):
        past_real = history[earlier, 0]
        past_imag = history[earlier, 1]
        volt_real = (
            volt_real
            + impedance[earlier + 1, 0] * past_real
            - impedance[earlier + 1, 1] * past_imag
        )
        volt_imag = (
            volt_imag
            + impedance[earlier + 1, 0] * past_imag
            + impedance[earlier + 1, 1] * past_real
        )
    back = contract("iack,ikon->oacn", jnp.stack([volt_real, volt_imag]), conjugate(third_table))
    second_own = group_index * second_part + jnp.arange(second_part, dtype=jnp.int32)
    depth_all = jnp.arange(N3, dtype=jnp.int32)
    cos_turn, sin_turn = rotation(second_own[None, :, None] * depth_all[None, None, :], plane_len)
    lift = turn(back, cos_turn, sin_turn)
    part = exchange(lift, "grp", 3, 2)
    spun = contract("iakb,ikon->oanb", part, conjugate(second_table))
    first_own = domain_index * first_part + jnp.arange(first_part, dtype=jnp.int32)
    cos_turn, sin_turn = rotation(
        first_own[:, None, None] * (second_freq[None, :, None] * N3 + depth_global[None, None, :]),
        cycle_len,
    )
    spin = turn(spun, cos_turn, sin_turn)
    inverse_factor = 1.0 / math.sqrt(cycle_len)
    part = exchange(spin, "dom", 2, 1)
    summed = contract("ikab,ikn->nab", part, conjugate(first_table)[:, :, 0, :])
    volt_part = summed * inverse_factor
    got = lax.all_to_all(volt_part.reshape(groups, R1, 128), "grp", 0, 0, tiled=True)
    got = got.reshape(per_row, 2, R1, 128)
    owned_volts = jnp.concatenate(
        [
            jnp.sum(
                jnp.where(lane_match, contract("sb,sl->bl", row_picker, got[:, h].reshape(-1, 128)), 0.0).reshape(
                    BUNCH_GRP, 128 // half, half
                ),
                axis=1,
            )
            for h in range(2)
        ],
        axis=1,
    )
    volt_rows = dom_sum(owned_volts, domains)
    drifted = energies - 0.5 * jnp.sin(two_pi * (positions - 0.5 * BINS) / BINS)
    positions_out, energies_out = kick_call(positions, drifted, volt_rows)
    return (positions_out, energies_out, spectrum)


def solution(mesh):
    placed = (
        P("grp", "dom"),
        P("grp", "dom"),
        P("grp"),
        P(None, None, "dom", "grp", None),
        P(None, None, "dom", "grp", None),
    )
    return jax.shard_map(
        on_device,
        mesh=mesh,
        in_specs=placed,
        out_specs=(P("grp", "dom"), P("grp", "dom"), P(None, "dom", "grp", None)),
        check_vma=False,
    )
```

```python
import math

import jax
import jax.numpy as jnp
from jax import lax
from jax.sharding import PartitionSpec as P
from jax.experimental import pallas as pl
from jax.experimental.pallas import tpu as pltpu

BINS = 32
N3 = 256
R1 = 8
R2 = 8
HIST = 2
BUNCH_GRP = 704
P_DEV = 256


highest = lax.Precision.HIGHEST
two_pi = 2.0 * math.pi
HALF_LOG2E = -0.5 / math.log(2.0)


def kernel_table(places):
    centers = jnp.arange(BINS, dtype=jnp.float32) + 0.5
    offset = places[:, None, :] - centers[None, :, None]
    return jnp.exp(-0.5 * offset * offset)


def dft_tables(length):
    series = jnp.arange(length, dtype=jnp.int32)
    windings = series[:, None] * series[None, :] % length
    angles = windings.astype(jnp.float32) * (two_pi / length)
    return (jnp.cos(angles), jnp.sin(angles))


def rotation(windings, modulus):
    angles = (windings % modulus).astype(jnp.float32) * (two_pi / modulus)
    return (jnp.cos(angles), jnp.sin(angles))


def contract(pattern, operand, matrix):
    return jnp.einsum(pattern, operand, matrix, precision=highest)


def block_table(length):
    cos_t, sin_t = dft_tables(length)
    return jnp.stack([jnp.stack([cos_t, -sin_t], axis=1), jnp.stack([sin_t, cos_t], axis=1)])


def conjugate(table):
    return table * jnp.array([1.0, -1.0], jnp.float32)[None, None, :, None] * jnp.array(
        [1.0, -1.0], jnp.float32
    )[:, None, None, None]


def turn(pair, cos_t, sin_t):
    return jnp.stack([pair[0] * cos_t - pair[1] * sin_t, pair[0] * sin_t + pair[1] * cos_t])


def exchange(x, axis_name, split_axis, concat_axis):
    count = lax.axis_size(axis_name)
    front = jnp.moveaxis(x, split_axis, 0)
    rest = front.shape[1:]
    piece = (front.shape[0] // count,) + rest
    sent = front.reshape(count, -1, 128)
    got = lax.all_to_all(sent, axis_name, 0, 0, tiled=True).reshape((count,) + piece)
    got = jnp.moveaxis(got, 1, split_axis + 1)
    got = jnp.moveaxis(got, 0, concat_axis)
    shape = list(x.shape)
    shape[split_axis] //= count
    shape[concat_axis] *= count
    return got.reshape(shape)


def dom_sum(rows, domains):
    chunk = rows.shape[0] // domains
    pieces = lax.all_to_all(rows.reshape(domains, -1, 128), "dom", 0, 0, tiled=True)
    mine = jnp.sum(pieces, axis=0)
    spread = jnp.broadcast_to(mine[None], (domains,) + mine.shape)
    return lax.all_to_all(spread, "dom", 0, 0, tiled=True).reshape(rows.shape)


KICK_ROWS = 352
SUB_ROWS = 32


def kick_kernel(pos_ref, drift_ref, volt_ref, pos_out, en_out):
    def sub_block(i, carry):
        rows = pl.ds(pl.multiple_of(i * SUB_ROWS, SUB_ROWS), SUB_ROWS)
        place = pos_ref[rows, :]
        volts = volt_ref[rows, :]
        weighted = jnp.zeros_like(place)
        norm = jnp.zeros_like(place)
        for j in range(BINS):
            offset = place - (j + 0.5)
            table = jnp.exp2(offset * offset * HALF_LOG2E)
            weighted = weighted + table * volts[:, j : j + 1]
            norm = norm + table
        energy = drift_ref[rows, :] - weighted / norm
        en_out[rows, :] = energy
        pos_out[rows, :] = place + 0.25 * energy
        return carry

    lax.fori_loop(0, KICK_ROWS // SUB_ROWS, sub_block, 0)


def kick_call(positions, drifted, volt_rows):
    bunches, width = positions.shape
    wide = pl.BlockSpec((KICK_ROWS, width), lambda i: (i, 0))
    narrow = pl.BlockSpec((KICK_ROWS, BINS), lambda i: (i, 0))
    shape = jax.ShapeDtypeStruct(positions.shape, jnp.float32)
    return pl.pallas_call(
        kick_kernel,
        grid=(bunches // KICK_ROWS,),
        in_specs=[wide, wide, narrow],
        out_specs=[wide, wide],
        out_shape=[shape, shape],
        cost_estimate=pl.CostEstimate(
            flops=12 * bunches * width * BINS,
            transcendentals=bunches * width * BINS,
            bytes_accessed=4 * bunches * (4 * width + BINS),
        ),
    )(positions, drifted, volt_rows)


def on_device(positions, energies, bucket, impedance, history):
    groups = lax.axis_size("grp")
    domains = lax.axis_size("dom")
    group_index = lax.axis_index("grp")
    domain_index = lax.axis_index("dom")
    first_len = R1 * groups
    second_len = R2 * domains
    cycle_len = first_len * second_len * N3
    plane_len = second_len * N3
    depth_len = N3 // groups
    first_part = first_len // domains
    second_part = second_len // groups
    per_row = N3 // BINS
    row_buckets = second_len * per_row
    own_rows = R2 * per_row
    partial_value = jnp.sum(kernel_table(positions), axis=2) / float(P_DEV * domains)
    first_row = bucket // row_buckets
    within = bucket % row_buckets
    owner_dom = within // own_rows
    owned_here = owner_dom == domain_index
    slot = jnp.where(owned_here, first_row * own_rows + within - owner_dom * own_rows, -1)
    picker = (slot[None, :] == jnp.arange(R1 * own_rows, dtype=jnp.int32)[:, None]).astype(jnp.float32)
    totals = dom_sum(partial_value, domains)
    in_row = within % per_row
    row_key = jnp.where(owned_here, in_row * R1 + first_row, -1)
    row_picker = (row_key[None, :] == jnp.arange(per_row * R1, dtype=jnp.int32)[:, None]).astype(jnp.float32)
    lane_slot = (within - owner_dom * own_rows) // per_row
    half = BINS // 2
    lane_match = lane_slot[:, None] == (jnp.arange(128, dtype=jnp.int32) // half)[None, :]
    halves = [
        contract(
            "sb,bl->sl",
            row_picker,
            jnp.where(lane_match, jnp.tile(totals[:, h * half : (h + 1) * half], (1, 128 // half)), 0.0),
        ).reshape(per_row, R1, 128)
        for h in range(2)
    ]
    send = jnp.stack(halves, axis=1).reshape(groups, R1, 128)
    first_table = block_table(first_len)
    second_table = block_table(second_len)
    third_table = block_table(N3)
    received = lax.all_to_all(send, "grp", 0, 0, tiled=True).reshape(first_len, R2, depth_len)
    rows = contract("nab,nok->oabk", received, first_table[0])
    second_global = domain_index * R2 + jnp.arange(R2, dtype=jnp.int32)
    depth_global = group_index * depth_len + jnp.arange(depth_len, dtype=jnp.int32)
    first_freq = jnp.arange(first_len, dtype=jnp.int32)
    cos_turn, sin_turn = rotation(
        first_freq[None, None, :]
        * (second_global[:, None, None] * N3 + depth_global[None, :, None]),
        cycle_len,
    )
    twist = turn(rows, cos_turn, -sin_turn)
    part = exchange(twist, "dom", 3, 1)
    cols = contract("inbk,inom->obkm", part, second_table)
    second_freq = jnp.arange(second_len, dtype=jnp.int32)
    cos_turn, sin_turn = rotation(
        depth_global[:, None, None] * second_freq[None, None, :], plane_len
    )
    turned = turn(cols, cos_turn, -sin_turn)
    past_real = impedance[1, 0] * history[0, 0] - impedance[1, 1] * history[0, 1]
    past_imag = impedance[1, 0] * history[0, 1] + impedance[1, 1] * history[0, 0]
    for earlier in range(1, HIST):
        past_real = past_real + (
            impedance[earlier + 1, 0] * history[earlier, 0] - impedance[earlier + 1, 1] * history[earlier, 1]
        )
        past_imag = past_imag + (
            impedance[earlier + 1, 0] * history[earlier, 1] + impedance[earlier + 1, 1] * history[earlier, 0]
        )
    past_real, past_imag, turned = lax.optimization_barrier((past_real, past_imag, turned))
    part = exchange(turned, "grp", 3, 1)
    full = contract("inac,inok->oack", part, third_table)
    norm_factor = 1.0 / math.sqrt(BUNCH_GRP * groups)
    spectrum = full * norm_factor
    spec_real = spectrum[0]
    spec_imag = spectrum[1]
    volt_real = impedance[0, 0] * spec_real - impedance[0, 1] * spec_imag + past_real
    volt_imag = impedance[0, 0] * spec_imag + impedance[0, 1] * spec_real + past_imag
    back = contract("iack,ikon->oacn", jnp.stack([volt_real, volt_imag]), conjugate(third_table))
    second_own = group_index * second_part + jnp.arange(second_part, dtype=jnp.int32)
    depth_all = jnp.arange(N3, dtype=jnp.int32)
    cos_turn, sin_turn = rotation(second_own[None, :, None] * depth_all[None, None, :], plane_len)
    lift = turn(back, cos_turn, sin_turn)
    part = exchange(lift, "grp", 3, 2)
    spun = contract("iakb,ikon->oanb", part, conjugate(second_table))
    first_own = domain_index * first_part + jnp.arange(first_part, dtype=jnp.int32)
    cos_turn, sin_turn = rotation(
        first_own[:, None, None] * (second_freq[None, :, None] * N3 + depth_global[None, None, :]),
        cycle_len,
    )
    spin = turn(spun, cos_turn, sin_turn)
    inverse_factor = 1.0 / math.sqrt(cycle_len)
    part = exchange(spin, "dom", 2, 1)
    summed = contract("ikab,ikn->nab", part, conjugate(first_table)[:, :, 0, :])
    volt_part = summed * inverse_factor
    volt_slab = exchange(volt_part, "grp", 0, 2).reshape(
        R1 * own_rows, BINS
    )
    owned_volts = contract("sb,sj->bj", picker, volt_slab)
    volt_rows = dom_sum(owned_volts, domains)
    drifted = energies - 0.5 * jnp.sin(two_pi * (positions - 0.5 * BINS) / BINS)
    positions_out, energies_out = kick_call(positions, drifted, volt_rows)
    return (positions_out, energies_out, spectrum)


def solution(mesh):
    placed = (
        P("grp", "dom"),
        P("grp", "dom"),
        P("grp"),
        P(None, None, "dom", "grp", None),
        P(None, None, "dom", "grp", None),
    )
    return jax.shard_map(
        on_device,
        mesh=mesh,
        in_specs=placed,
        out_specs=(P("grp", "dom"), P("grp", "dom"), P(None, "dom", "grp", None)),
        check_vma=False,
    )
```
